128 devices in a mesh: dom: 16 (over y_lo, z, core), mem: 8 (over y_hi, x).
Axes of the slice: x: 4, y: 4 (y_hi: 2, y_lo: 2; y = y_hi * 2 + y_lo), z: 4, core: 2. Of those that a mesh axis runs over, the one named last changes fastest.
Arguments:
- perturbations: float32 [64, 8, 128, 512], P('mem', None, 'dom'), may hold values from -50 to 50
- trajectory: bfloat16 [2, 5, 8, 128, 512], P(None, None, 'mem', 'dom'), may hold values from 0 to 1, as said below
Outputs:
- ritz: float32 [64, 8, 128, 512], P('mem', None, 'dom')
- projected: float32 [64, 64], replicated
The draws below stay inside these ranges and needn't reach their ends.
Inputs may be any that keep to these rules, and one draw needn't show every extreme that they name: `trajectory`: every coefficient is nonnegative and the five coefficients of a cell sum to one up to rounding.
All inputs are finite; a program needn't handle non-finite values.
Results may differ from the reference program's by a relative error of at most 0.0003.
Values may be sent and summed in bfloat16 or wider, within the bound.
No kernel may reach another device: no remote copies, remote signals or barrier semaphores. Data moves between devices by JAX's collectives and lax.ppermute only.
A program may use at most 64 MiB of HBM per device.

```python
import jax
import jax.numpy as jnp
from jax import lax

M = 64
LEV = 8
STEPS = 2
NY = 512
NX = 128
NCELLS = 524288


def draw_perturbations(key, part):
    first = jax.random.fold_in(key, 0)
    noise = jax.random.normal(first, (M, LEV, NX, NY), jnp.float32)
    mixed = noise + 0.5 * jnp.roll(noise, -1, 0) + 0.25 * jnp.roll(noise, -3, 0)
    ramp = 1.0 + 2.0 * jnp.arange(NX, dtype=jnp.float32) / max(NX - 1, 1)
    return (mixed * ramp[None, None, :, None] / 1.15).astype(jnp.float32)


def draw_trajectory(key, part):
    keys = jax.random.split(key, 4)
    shape = (STEPS, LEV, NX, NY)
    speed_x = jax.random.uniform(keys[0], shape, jnp.float32, -0.2, 0.2)
    speed_y = jax.random.uniform(keys[1], shape, jnp.float32, -0.2, 0.2)
    diff_x = jax.random.uniform(keys[2], shape, jnp.float32, 0.1, 0.24)
    diff_y = jax.random.uniform(keys[3], shape, jnp.float32, 0.1, 0.24)
    centre = 1.0 - 2.0 * diff_x - 2.0 * diff_y
    west = diff_x + 0.5 * speed_x
    east = diff_x - 0.5 * speed_x
    south = diff_y + 0.5 * speed_y
    north = diff_y - 0.5 * speed_y
    stacked = jnp.stack([centre, west, east, south, north], axis=1)
    return jnp.clip(stacked, 0.0, 1.0).astype(jnp.bfloat16)


def setup_inputs(seed: int = 0) -> dict:
    seeds = jax.random.split(jax.random.key(seed), 3)
    return {
        "perturbations": draw_perturbations(jax.random.fold_in(seeds[2], 71), 0),
        "trajectory": draw_trajectory(jax.random.fold_in(seeds[2], 71), 0),
    }


def forward_step(field, coef):
    padded = jnp.pad(field, ((0, 0), (0, 0), (1, 1), (1, 1)))
    result = coef[0] * field + coef[1] * padded[:, :, :-2, 1:-1] + coef[2] * padded[:, :, 2:, 1:-1]
    return result + coef[3] * padded[:, :, 1:-1, :-2] + coef[4] * padded[:, :, 1:-1, 2:]

def adjoint_step(field, coef):

    def padded(term):
        return jnp.pad(coef[term] * field, ((0, 0), (0, 0), (1, 1), (1, 1)))
    result = coef[0] * field + padded(1)[:, :, 2:, 1:-1] + padded(2)[:, :, :-2, 1:-1]
    return result + padded(3)[:, :, 1:-1, 2:] + padded(4)[:, :, 1:-1, :-2]

def reference(perturbations, trajectory):
    coeffs = trajectory.astype(jnp.float32)
    field = perturbations
    for step in range(STEPS):
        field = forward_step(field, coeffs[step])
    for step in reversed(range(STEPS)):
        field = adjoint_step(field, coeffs[step])
    flat_v = perturbations.reshape(M, -1)
    flat_w = field.reshape(M, -1)
    hi = lax.Precision.HIGHEST
    gram = jnp.dot(flat_v, flat_v.T, precision=hi) / NCELLS
    projected = jnp.dot(flat_v, flat_w.T, precision=hi) / NCELLS
    factor = jnp.linalg.cholesky(gram)
    inverse = jax.scipy.linalg.cho_solve((factor, True), jnp.eye(M, dtype=jnp.float32))
    ritz = jnp.dot(inverse, flat_w, precision=hi)
    return (ritz.reshape(perturbations.shape), projected)
```

```python
import jax
import jax.numpy as jnp
from jax import lax
from jax.sharding import PartitionSpec as P

STEPS = 2


def halo_rows(low_src, high_src):
    count = lax.axis_size("dom")
    forward = [(i, i + 1) for i in range(count - 1)]
    backward = [(i + 1, i) for i in range(count - 1)]
    low = lax.ppermute(low_src, "dom", forward)
    high = lax.ppermute(high_src, "dom", backward)
    return low, high


def forward_step(field, coef):
    low, high = halo_rows(field[:, :, -1:, :], field[:, :, :1, :])
    padded = jnp.concatenate([low, field, high], axis=2)
    side = jnp.pad(field, ((0, 0), (0, 0), (0, 0), (1, 1)))
    result = coef[0] * field + coef[1] * padded[:, :, :-2, :] + coef[2] * padded[:, :, 2:, :]
    return result + coef[3] * side[:, :, :, :-2] + coef[4] * side[:, :, :, 2:]


def adjoint_step(field, coef):
    west = coef[1] * field
    east = coef[2] * field
    low, high = halo_rows(east[:, :, -1:, :], west[:, :, :1, :])
    west_p = jnp.concatenate([west, high], axis=2)[:, :, 1:, :]
    east_p = jnp.concatenate([low, east], axis=2)[:, :, :-1, :]
    south_term = jnp.pad(coef[3] * field, ((0, 0), (0, 0), (0, 0), (0, 1)))[:, :, :, 1:]
    north_term = jnp.pad(coef[4] * field, ((0, 0), (0, 0), (0, 0), (1, 0)))[:, :, :, :-1]
    return coef[0] * field + south_term + north_term + west_p + east_p


def invert(gram):
    factor = jnp.linalg.cholesky(gram)
    return jax.scipy.linalg.cho_solve((factor, True), jnp.eye(gram.shape[0], dtype=jnp.float32))


def body(perturbations, trajectory):
    groups = lax.axis_size("mem")
    v = lax.all_to_all(perturbations, "mem", 1, 0, tiled=True)
    coeffs = trajectory.astype(jnp.float32)
    field = v
    for step in range(STEPS):
        field = forward_step(field, coeffs[step])
    for step in reversed(range(STEPS)):
        field = adjoint_step(field, coeffs[step])
    members = v.shape[0]
    ncells_all = (
        perturbations.shape[1]
        * perturbations.shape[2]
        * perturbations.shape[3]
        * lax.axis_size("dom")
    )
    flat_v = v.reshape(members, -1)
    flat_w = field.reshape(members, -1)
    hi = lax.Precision.HIGHEST
    gram = jnp.dot(flat_v, flat_v.T, precision=hi)
    cross = jnp.dot(flat_v, flat_w.T, precision=hi)
    both = lax.psum(jnp.stack([gram, cross]), ("mem", "dom"))
    gram = both[0] / ncells_all
    projected = both[1] / ncells_all
    inverse = invert(gram)
    ritz = jnp.dot(inverse, flat_w, precision=hi).reshape(v.shape)
    ritz = lax.all_to_all(ritz, "mem", 0, 1, tiled=True)
    return (ritz, projected)


def solution(mesh):
    return jax.shard_map(
        body,
        mesh=mesh,
        in_specs=(P("mem", None, "dom", None), P(None, None, "mem", "dom", None)),
        out_specs=(P("mem", None, "dom", None), P()),
        check_vma=False,
    )
```

```python
import jax
import jax.numpy as jnp
from jax import lax
from jax.sharding import PartitionSpec as P

STEPS = 2


def halo(block, width, dim):
    count = lax.axis_size("dom")
    forward = [(i, i + 1) for i in range(count - 1)]
    backward = [(i + 1, i) for i in range(count - 1)]
    size = block.shape[dim]
    low = lax.ppermute(lax.slice_in_dim(block, size - width, size, axis=dim), "dom", forward)
    high = lax.ppermute(lax.slice_in_dim(block, 0, width, axis=dim), "dom", backward)
    return jnp.concatenate([low, block, high], axis=dim)


def shifted(x, offset, dim):
    pad = [(0, 0)] * x.ndim
    size = x.shape[dim]
    if offset > 0:
        pad[dim] = (0, offset)
        return lax.slice_in_dim(jnp.pad(x, pad), offset, offset + size, axis=dim)
    pad[dim] = (-offset, 0)
    return lax.slice_in_dim(jnp.pad(x, pad), 0, size, axis=dim)


def forward_step(field, coef):
    result = coef[0] * field + coef[1] * shifted(field, -1, 2) + coef[2] * shifted(field, 1, 2)
    return result + coef[3] * shifted(field, -1, 3) + coef[4] * shifted(field, 1, 3)


def adjoint_step(field, coef):
    result = coef[0] * field + shifted(coef[1] * field, 1, 2) + shifted(coef[2] * field, -1, 2)
    return result + shifted(coef[3] * field, 1, 3) + shifted(coef[4] * field, -1, 3)


def butterfly(x, axis):
    count = lax.axis_size(axis)
    bit = 1
    while bit < count:
        x = x + lax.ppermute(x, axis, [(i, i ^ bit) for i in range(count)])
        bit *= 2
    return x


def invert(gram):
    factor = jnp.linalg.cholesky(gram)
    return jax.scipy.linalg.cho_solve((factor, True), jnp.eye(gram.shape[0], dtype=jnp.float32))


def body(perturbations, trajectory):
    width = 2 * STEPS
    rows = perturbations.shape[2]
    assert width <= rows
    v = lax.all_to_all(perturbations, "mem", 1, 0, tiled=True)
    coeffs = halo(trajectory, width, 3).astype(jnp.float32)
    field = halo(v, width, 2)
    for step in range(STEPS):
        field = forward_step(field, coeffs[step])
    for step in reversed(range(STEPS)):
        field = adjoint_step(field, coeffs[step])
    field = field[:, :, width : width + rows, :]
    members = v.shape[0]
    ncells_all = (
        perturbations.shape[1]
        * perturbations.shape[2]
        * perturbations.shape[3]
        * lax.axis_size("dom")
    )
    flat_v = v.reshape(members, -1)
    flat_w = field.reshape(members, -1)
    hi = lax.Precision.HIGHEST
    gram = jnp.dot(flat_v, flat_v.T, precision=hi)
    cross = jnp.dot(flat_v, flat_w.T, precision=hi)
    both = butterfly(butterfly(jnp.stack([gram, cross]), "mem"), "dom")
    gram = both[0] / ncells_all
    projected = both[1] / ncells_all
    inverse = invert(gram)
    ritz = jnp.dot(inverse, flat_w, precision=hi).reshape(v.shape)
    ritz = lax.all_to_all(ritz, "mem", 0, 1, tiled=True)
    return (ritz, projected)


def solution(mesh):
    return jax.shard_map(
        body,
        mesh=mesh,
        in_specs=(P("mem", None, "dom", None), P(None, None, "mem", "dom", None)),
        out_specs=(P("mem", None, "dom", None), P()),
        check_vma=False,
    )
```

```python
import jax
import jax.numpy as jnp
from jax import lax
from jax.sharding import PartitionSpec as P

STEPS = 2


def halo(block, width, dim):
    count = lax.axis_size("dom")
    forward = [(i, i + 1) for i in range(count - 1)]
    backward = [(i + 1, i) for i in range(count - 1)]
    size = block.shape[dim]
    low = lax.ppermute(lax.slice_in_dim(block, size - width, size, axis=dim), "dom", forward)
    high = lax.ppermute(lax.slice_in_dim(block, 0, width, axis=dim), "dom", backward)
    return jnp.concatenate([low, block, high], axis=dim)


def shifted(x, offset, dim):
    pad = [(0, 0)] * x.ndim
    size = x.shape[dim]
    if offset > 0:
        pad[dim] = (0, offset)
        return lax.slice_in_dim(jnp.pad(x, pad), offset, offset + size, axis=dim)
    pad[dim] = (-offset, 0)
    return lax.slice_in_dim(jnp.pad(x, pad), 0, size, axis=dim)


def forward_step(field, coef):
    result = coef[0] * field + coef[1] * shifted(field, -1, 2) + coef[2] * shifted(field, 1, 2)
    return result + coef[3] * shifted(field, -1, 3) + coef[4] * shifted(field, 1, 3)


def adjoint_step(field, coef):
    result = coef[0] * field + shifted(coef[1] * field, 1, 2) + shifted(coef[2] * field, -1, 2)
    return result + shifted(coef[3] * field, 1, 3) + shifted(coef[4] * field, -1, 3)


def butterfly_bits():
    bits = []
    for axis in ("mem", "dom"):
        bit = 1
        while bit < lax.axis_size(axis):
            bits.append((axis, bit))
            bit *= 2
    return bits


def exchange(x, axis, bit):
    count = lax.axis_size(axis)
    return x + lax.ppermute(x, axis, [(i, i ^ bit) for i in range(count)])


def invert(gram):
    factor = jnp.linalg.cholesky(gram)
    return jax.scipy.linalg.cho_solve((factor, True), jnp.eye(gram.shape[0], dtype=jnp.float32))


def body(perturbations, trajectory):
    width = 2 * STEPS
    rows = perturbations.shape[2]
    assert width <= rows
    coeffs = halo(trajectory, width, 3).astype(jnp.float32)
    v = lax.all_to_all(perturbations, "mem", 1, 0, tiled=True)
    members = v.shape[0]
    ncells_all = (
        perturbations.shape[1]
        * perturbations.shape[2]
        * perturbations.shape[3]
        * lax.axis_size("dom")
    )
    hi = lax.Precision.HIGHEST
    flat_v = v.reshape(members, -1)
    gram = jnp.dot(flat_v, flat_v.T, precision=hi)
    bits = butterfly_bits()
    done = 0
    field = halo(v, width, 2)
    plan = [(forward_step, s) for s in range(STEPS)]
    plan += [(adjoint_step, s) for s in reversed(range(STEPS))]
    for apply, step in plan:
        field = apply(field, coeffs[step])
        if done < len(bits):
            gram = exchange(gram, *bits[done])
            done += 1
        gram, field = lax.optimization_barrier((gram, field))
    field = field[:, :, width : width + rows, :]
    flat_w = field.reshape(members, -1)
    cross = jnp.dot(flat_v, flat_w.T, precision=hi)
    both = jnp.stack([gram, cross])
    for axis, bit in bits[done:]:
        both = exchange(both, axis, bit)
    gram, cross = both[0], both[1]
    for axis, bit in bits[:done]:
        cross = exchange(cross, axis, bit)
    inverse = invert(gram / ncells_all)
    projected = cross / ncells_all
    ritz = jnp.dot(inverse, flat_w, precision=hi).reshape(v.shape)
    ritz = lax.all_to_all(ritz, "mem", 0, 1, tiled=True)
    return (ritz, projected)


def solution(mesh):
    return jax.shard_map(
        body,
        mesh=mesh,
        in_specs=(P("mem", None, "dom", None), P(None, None, "mem", "dom", None)),
        out_specs=(P("mem", None, "dom", None), P()),
        check_vma=False,
    )
```

```python
import jax
import jax.numpy as jnp
from jax import lax
from jax.sharding import PartitionSpec as P

STEPS = 2


def halo(block, width, dim):
    count = lax.axis_size("dom")
    forward = [(i, i + 1) for i in range(count - 1)]
    backward = [(i + 1, i) for i in range(count - 1)]
    size = block.shape[dim]
    low = lax.ppermute(lax.slice_in_dim(block, size - width, size, axis=dim), "dom", forward)
    high = lax.ppermute(lax.slice_in_dim(block, 0, width, axis=dim), "dom", backward)
    return jnp.concatenate([low, block, high], axis=dim)


def shifted(x, offset, dim):
    pad = [(0, 0)] * x.ndim
    size = x.shape[dim]
    if offset > 0:
        pad[dim] = (0, offset)
        return lax.slice_in_dim(jnp.pad(x, pad), offset, offset + size, axis=dim)
    pad[dim] = (-offset, 0)
    return lax.slice_in_dim(jnp.pad(x, pad), 0, size, axis=dim)


def forward_step(field, coef):
    result = coef[0] * field + coef[1] * shifted(field, -1, 2) + coef[2] * shifted(field, 1, 2)
    return result + coef[3] * shifted(field, -1, 3) + coef[4] * shifted(field, 1, 3)


def adjoint_step(field, coef):
    result = coef[0] * field + shifted(coef[1] * field, 1, 2) + shifted(coef[2] * field, -1, 2)
    return result + shifted(coef[3] * field, 1, 3) + shifted(coef[4] * field, -1, 3)


def butterfly_bits():
    bits = []
    for axis in ("mem", "dom"):
        bit = 1
        while bit < lax.axis_size(axis):
            bits.append((axis, bit))
            bit *= 2
    return bits


def exchange(x, axis, bit):
    count = lax.axis_size(axis)
    return x + lax.ppermute(x, axis, [(i, i ^ bit) for i in range(count)])


def invert_beside(gram, extra, bits):
    factor = jnp.linalg.cholesky(gram)
    if bits:
        extra = exchange(extra, *bits.pop(0))
    factor, extra = lax.optimization_barrier((factor, extra))
    eye = jnp.eye(gram.shape[0], dtype=jnp.float32)
    inverse = jax.scipy.linalg.cho_solve((factor, True), eye)
    if bits:
        extra = exchange(extra, *bits.pop(0))
    inverse, extra = lax.optimization_barrier((inverse, extra))
    return inverse, extra


def body(perturbations, trajectory):
    width = 2 * STEPS
    rows = perturbations.shape[2]
    assert width <= rows
    coeffs = halo(trajectory, width, 3).astype(jnp.float32)
    v = lax.all_to_all(perturbations, "mem", 1, 0, tiled=True)
    members = v.shape[0]
    ncells_all = (
        perturbations.shape[1]
        * perturbations.shape[2]
        * perturbations.shape[3]
        * lax.axis_size("dom")
    )
    hi = lax.Precision.HIGHEST
    flat_v = v.reshape(members, -1)
    gram = jnp.dot(flat_v, flat_v.T, precision=hi)
    pending = butterfly_bits()
    done = []

    def tick(acc, field):
        if pending:
            bit = pending.pop(0)
            acc = exchange(acc, *bit)
            done.append(bit)
        return lax.optimization_barrier((acc, field))

    gram, field = tick(gram, halo(v, width, 2))
    for step in range(STEPS):
        gram, field = tick(gram, forward_step(field, coeffs[step]))
    flat_z = field[:, :, width : width + rows, :].reshape(members, -1)
    cross = jnp.dot(flat_z, flat_z.T, precision=hi)
    both = jnp.stack([gram, cross])
    cross_bits = list(done)
    for step in reversed(range(STEPS)):
        both, field = tick(both, adjoint_step(field, coeffs[step]))
    while pending:
        both = exchange(both, *pending.pop(0))
    gram, cross = both[0], both[1]
    field = field[:, :, width : width + rows, :]
    flat_w = field.reshape(members, -1)
    inverse, cross = invert_beside(gram / ncells_all, cross, cross_bits)
    ritz = jnp.dot(inverse, flat_w, precision=hi)
    for axis, bit in cross_bits:
        cross = exchange(cross, axis, bit)
    projected = cross / ncells_all
    ritz = lax.all_to_all(ritz.reshape(v.shape), "mem", 0, 1, tiled=True)
    return (ritz, projected)


def solution(mesh):
    return jax.shard_map(
        body,
        mesh=mesh,
        in_specs=(P("mem", None, "dom", None), P(None, None, "mem", "dom", None)),
        out_specs=(P("mem", None, "dom", None), P()),
        check_vma=False,
    )
```

```python
import jax
import jax.numpy as jnp
from jax import lax
from jax.experimental import pallas as pl
from jax.experimental.pallas import tpu as pltpu
from jax.sharding import PartitionSpec as P

STEPS = 2


def halo(block, width, dim):
    count = lax.axis_size("dom")
    forward = [(i, i + 1) for i in range(count - 1)]
    backward = [(i + 1, i) for i in range(count - 1)]
    size = block.shape[dim]
    low = lax.ppermute(lax.slice_in_dim(block, size - width, size, axis=dim), "dom", forward)
    high = lax.ppermute(lax.slice_in_dim(block, 0, width, axis=dim), "dom", backward)
    return jnp.concatenate([low, block, high], axis=dim)


def shifted(x, offset, dim):
    pad = [(0, 0)] * x.ndim
    size = x.shape[dim]
    if offset > 0:
        pad[dim] = (0, offset)
        return lax.slice_in_dim(jnp.pad(x, pad), offset, offset + size, axis=dim)
    pad[dim] = (-offset, 0)
    return lax.slice_in_dim(jnp.pad(x, pad), 0, size, axis=dim)


def forward_step(field, coef):
    result = coef[0] * field + coef[1] * shifted(field, -1, 2) + coef[2] * shifted(field, 1, 2)
    return result + coef[3] * shifted(field, -1, 3) + coef[4] * shifted(field, 1, 3)


def adjoint_step(field, coef):
    result = coef[0] * field + shifted(coef[1] * field, 1, 2) + shifted(coef[2] * field, -1, 2)
    return result + shifted(coef[3] * field, 1, 3) + shifted(coef[4] * field, -1, 3)


def butterfly_bits():
    bits = []
    for axis in ("mem", "dom"):
        bit = 1
        while bit < lax.axis_size(axis):
            bits.append((axis, bit))
            bit *= 2
    return bits


def exchange(x, axis, bit):
    count = lax.axis_size(axis)
    return x + lax.ppermute(x, axis, [(i, i ^ bit) for i in range(count)])


def chol_inv_kernel(g_ref, x_ref, a_ref):
    n = g_ref.shape[0]
    a_ref[...] = g_ref[...]
    rows = lax.broadcasted_iota(jnp.int32, (n, n), 0)
    cols = lax.broadcasted_iota(jnp.int32, (n, n), 1)
    x_ref[...] = jnp.where(rows == cols, 1.0, 0.0).astype(jnp.float32)
    lane = lax.broadcasted_iota(jnp.int32, (1, n), 1)
    sub = lax.broadcasted_iota(jnp.int32, (n, 1), 0)

    def step(k, carry):
        a = a_ref[...]
        row = a_ref[pl.ds(k, 1), :]
        pivot = jnp.sum(jnp.where(lane == k, row, 0.0), axis=1, keepdims=True)
        root = jnp.sqrt(pivot)
        col = jnp.sum(jnp.where(cols == k, a, 0.0), axis=1, keepdims=True)
        below = jnp.where(sub > k, col / root, 0.0)
        right = jnp.where(lane > k, row / root, 0.0)
        a_ref[...] = a - below * right
        xrow = x_ref[pl.ds(k, 1), :] / root
        x_ref[pl.ds(k, 1), :] = xrow
        x_ref[...] = x_ref[...] - below * xrow
        return carry

    lax.fori_loop(0, n, step, 0)


def lower_inverse(gram):
    n = gram.shape[0]
    return pl.pallas_call(
        chol_inv_kernel,
        out_shape=jax.ShapeDtypeStruct((n, n), jnp.float32),
        scratch_shapes=[pltpu.VMEM((n, n), jnp.float32)],
    )(gram)


def invert_beside(gram, extra, bits):
    solved = lower_inverse(gram)
    if bits:
        extra = exchange(extra, *bits.pop(0))
    solved, extra = lax.optimization_barrier((solved, extra))
    inverse = jnp.dot(solved.T, solved, precision=lax.Precision.HIGHEST)
    if bits:
        extra = exchange(extra, *bits.pop(0))
    inverse, extra = lax.optimization_barrier((inverse, extra))
    return inverse, extra


def body(perturbations, trajectory):
    width = 2 * STEPS
    rows = perturbations.shape[2]
    assert width <= rows
    coeffs = halo(trajectory, width, 3).astype(jnp.float32)
    v = lax.all_to_all(perturbations, "mem", 1, 0, tiled=True)
    members = v.shape[0]
    ncells_all = (
        perturbations.shape[1]
        * perturbations.shape[2]
        * perturbations.shape[3]
        * lax.axis_size("dom")
    )
    hi = lax.Precision.HIGHEST
    flat_v = v.reshape(members, -1)
    gram = jnp.dot(flat_v, flat_v.T, precision=hi)
    pending = butterfly_bits()
    done = []

    def tick(acc, field):
        if pending:
            bit = pending.pop(0)
            acc = exchange(acc, *bit)
            done.append(bit)
        return lax.optimization_barrier((acc, field))

    gram, field = tick(gram, halo(v, width, 2))
    for step in range(STEPS):
        gram, field = tick(gram, forward_step(field, coeffs[step]))
    flat_z = field[:, :, width : width + rows, :].reshape(members, -1)
    cross = jnp.dot(flat_z, flat_z.T, precision=hi)
    both = jnp.stack([gram, cross])
    cross_bits = list(done)
    for step in reversed(range(STEPS)):
        both, field = tick(both, adjoint_step(field, coeffs[step]))
    while pending:
        both = exchange(both, *pending.pop(0))
    gram, cross = both[0], both[1]
    field = field[:, :, width : width + rows, :]
    flat_w = field.reshape(members, -1)
    inverse, cross = invert_beside(gram / ncells_all, cross, cross_bits)
    ritz = jnp.dot(inverse, flat_w, precision=hi)
    for axis, bit in cross_bits:
        cross = exchange(cross, axis, bit)
    projected = cross / ncells_all
    ritz = lax.all_to_all(ritz.reshape(v.shape), "mem", 0, 1, tiled=True)
    return (ritz, projected)


def solution(mesh):
    return jax.shard_map(
        body,
        mesh=mesh,
        in_specs=(P("mem", None, "dom", None), P(None, None, "mem", "dom", None)),
        out_specs=(P("mem", None, "dom", None), P()),
        check_vma=False,
    )
```

```python
import jax
import jax.numpy as jnp
from jax import lax
from jax.experimental import pallas as pl
from jax.experimental.pallas import tpu as pltpu
from jax.sharding import PartitionSpec as P

STEPS = 2


def halo(block, width, dim):
    count = lax.axis_size("dom")
    forward = [(i, i + 1) for i in range(count - 1)]
    backward = [(i + 1, i) for i in range(count - 1)]
    size = block.shape[dim]
    low = lax.ppermute(lax.slice_in_dim(block, size - width, size, axis=dim), "dom", forward)
    high = lax.ppermute(lax.slice_in_dim(block, 0, width, axis=dim), "dom", backward)
    return jnp.concatenate([low, block, high], axis=dim)


def shifted(x, offset, dim):
    pad = [(0, 0)] * x.ndim
    size = x.shape[dim]
    if offset > 0:
        pad[dim] = (0, offset)
        return lax.slice_in_dim(jnp.pad(x, pad), offset, offset + size, axis=dim)
    pad[dim] = (-offset, 0)
    return lax.slice_in_dim(jnp.pad(x, pad), 0, size, axis=dim)


def forward_step(field, coef):
    result = coef[0] * field + coef[1] * shifted(field, -1, 2) + coef[2] * shifted(field, 1, 2)
    return result + coef[3] * shifted(field, -1, 3) + coef[4] * shifted(field, 1, 3)


def adjoint_step(field, coef):
    result = coef[0] * field + shifted(coef[1] * field, 1, 2) + shifted(coef[2] * field, -1, 2)
    return result + shifted(coef[3] * field, 1, 3) + shifted(coef[4] * field, -1, 3)


def butterfly_bits():
    bits = []
    for axis in ("mem", "dom"):
        bit = 1
        while bit < lax.axis_size(axis):
            bits.append((axis, bit))
            bit *= 2
    return bits


def exchange(x, axis, bit):
    count = lax.axis_size(axis)
    return x + lax.ppermute(x, axis, [(i, i ^ bit) for i in range(count)])


def chol_inv_kernel(g_ref, x_ref, a_ref):
    n = g_ref.shape[0]
    a_ref[...] = g_ref[...]
    rows = lax.broadcasted_iota(jnp.int32, (n, n), 0)
    cols = lax.broadcasted_iota(jnp.int32, (n, n), 1)
    x_ref[...] = jnp.where(rows == cols, 1.0, 0.0).astype(jnp.float32)
    lane = lax.broadcasted_iota(jnp.int32, (1, n), 1)
    sub = lax.broadcasted_iota(jnp.int32, (n, 1), 0)

    def step(k, carry):
        a = a_ref[...]
        row = a_ref[pl.ds(k, 1), :]
        pivot = jnp.sum(jnp.where(lane == k, row, 0.0), axis=1, keepdims=True)
        root = jnp.sqrt(pivot)
        col = jnp.sum(jnp.where(cols == k, a, 0.0), axis=1, keepdims=True)
        below = jnp.where(sub > k, col / root, 0.0)
        right = jnp.where(lane > k, row / root, 0.0)
        a_ref[...] = a - below * right
        xrow = x_ref[pl.ds(k, 1), :] / root
        x_ref[pl.ds(k, 1), :] = xrow
        x_ref[...] = x_ref[...] - below * xrow
        return carry

    lax.fori_loop(0, n, step, 0)


def lower_inverse(gram):
    n = gram.shape[0]
    return pl.pallas_call(
        chol_inv_kernel,
        out_shape=jax.ShapeDtypeStruct((n, n), jnp.float32),
        scratch_shapes=[pltpu.VMEM((n, n), jnp.float32)],
    )(gram)


def invert_beside(gram, extra, bits):
    solved = lower_inverse(gram)
    if bits:
        extra = exchange(extra, *bits.pop(0))
    solved, extra = lax.optimization_barrier((solved, extra))
    inverse = jnp.dot(solved.T, solved, precision=lax.Precision.HIGHEST)
    return inverse, extra


def body(perturbations, trajectory):
    width = 2 * STEPS
    rows = perturbations.shape[2]
    assert width <= rows
    coeffs = halo(trajectory, width, 3).astype(jnp.float32)
    v = lax.all_to_all(perturbations, "mem", 1, 0, tiled=True)
    members = v.shape[0]
    ncells_all = (
        perturbations.shape[1]
        * perturbations.shape[2]
        * perturbations.shape[3]
        * lax.axis_size("dom")
    )
    hi = lax.Precision.HIGHEST
    flat_v = v.reshape(members, -1)
    gram = jnp.dot(flat_v, flat_v.T, precision=hi)
    pending = butterfly_bits()
    done = []

    def tick(acc, field):
        if pending:
            bit = pending.pop(0)
            acc = exchange(acc, *bit)
            done.append(bit)
        return lax.optimization_barrier((acc, field))

    gram, field = tick(gram, halo(v, width, 2))
    for step in range(STEPS):
        gram, field = tick(gram, forward_step(field, coeffs[step]))
    flat_z = field[:, :, width : width + rows, :].reshape(members, -1)
    cross = jnp.dot(flat_z, flat_z.T, precision=hi)
    both = jnp.stack([gram, cross])
    cross_bits = list(done)
    for step in reversed(range(STEPS)):
        both, field = tick(both, adjoint_step(field, coeffs[step]))
    while pending:
        both = exchange(both, *pending.pop(0))
    gram, cross = both[0], both[1]
    field = field[:, :, width : width + rows, :]
    flat_w = field.reshape(members, -1)
    inverse, cross = invert_beside(gram / ncells_all, cross, cross_bits)
    ritz = jnp.dot(inverse, flat_w, precision=hi)
    for axis, bit in cross_bits:
        cross = exchange(cross, axis, bit)
    projected = cross / ncells_all
    ritz = lax.all_to_all(ritz.reshape(v.shape), "mem", 0, 1, tiled=True)
    return (ritz, projected)


def solution(mesh):
    return jax.shard_map(
        body,
        mesh=mesh,
        in_specs=(P("mem", None, "dom", None), P(None, None, "mem", "dom", None)),
        out_specs=(P("mem", None, "dom", None), P()),
        check_vma=False,
    )
```

```python
import functools

import jax
import jax.numpy as jnp
from jax import lax
from jax.experimental import pallas as pl
from jax.sharding import PartitionSpec as P

STEPS = 2


def halo(block, width, dim):
    count = lax.axis_size("dom")
    forward = [(i, i + 1) for i in range(count - 1)]
    backward = [(i + 1, i) for i in range(count - 1)]
    size = block.shape[dim]
    low = lax.ppermute(lax.slice_in_dim(block, size - width, size, axis=dim), "dom", forward)
    high = lax.ppermute(lax.slice_in_dim(block, 0, width, axis=dim), "dom", backward)
    return jnp.concatenate([low, block, high], axis=dim)


def shifted(x, offset, dim):
    pad = [(0, 0)] * x.ndim
    size = x.shape[dim]
    if offset > 0:
        pad[dim] = (0, offset)
        return lax.slice_in_dim(jnp.pad(x, pad), offset, offset + size, axis=dim)
    pad[dim] = (-offset, 0)
    return lax.slice_in_dim(jnp.pad(x, pad), 0, size, axis=dim)


def forward_step(field, coef):
    result = coef[0] * field + coef[1] * shifted(field, -1, 2) + coef[2] * shifted(field, 1, 2)
    return result + coef[3] * shifted(field, -1, 3) + coef[4] * shifted(field, 1, 3)


def adjoint_step(field, coef):
    result = coef[0] * field + shifted(coef[1] * field, 1, 2) + shifted(coef[2] * field, -1, 2)
    return result + shifted(coef[3] * field, 1, 3) + shifted(coef[4] * field, -1, 3)


def butterfly_bits():
    bits = []
    for axis in ("mem", "dom"):
        bit = 1
        while bit < lax.axis_size(axis):
            bits.append((axis, bit))
            bit *= 2
    return bits


def exchange(x, axis, bit):
    count = lax.axis_size(axis)
    return x + lax.ppermute(x, axis, [(i, i ^ bit) for i in range(count)])


def chol_inv_kernel(first, last, a_in, x_in, a_ref, x_ref):
    n = a_in.shape[0]
    a_ref[...] = a_in[...]
    x_ref[...] = x_in[...]
    cols = lax.broadcasted_iota(jnp.int32, (n, n), 1)
    lane = lax.broadcasted_iota(jnp.int32, (1, n), 1)
    sub = lax.broadcasted_iota(jnp.int32, (n, 1), 0)

    def step(k, carry):
        a = a_ref[...]
        row = a_ref[pl.ds(k, 1), :]
        pivot = jnp.sum(jnp.where(lane == k, row, 0.0), axis=1, keepdims=True)
        root = jnp.sqrt(pivot)
        col = jnp.sum(jnp.where(cols == k, a, 0.0), axis=1, keepdims=True)
        below = jnp.where(sub > k, col / root, 0.0)
        right = jnp.where(lane > k, row / root, 0.0)
        a_ref[...] = a - below * right
        xrow = x_ref[pl.ds(k, 1), :] / root
        x_ref[pl.ds(k, 1), :] = xrow
        x_ref[...] = x_ref[...] - below * xrow
        return carry

    lax.fori_loop(first, last, step, 0)


def cholesky_steps(a, x, first, last):
    n = a.shape[0]
    shape = jax.ShapeDtypeStruct((n, n), jnp.float32)
    return pl.pallas_call(
        functools.partial(chol_inv_kernel, first, last),
        out_shape=(shape, shape),
    )(a, x)


def invert_beside(gram, extra, bits):
    n = gram.shape[0]
    bounds = [0, n // 2, n]
    a, x = gram, jnp.eye(n, dtype=jnp.float32)
    for first, last in zip(bounds[:-1], bounds[1:]):
        a, x = cholesky_steps(a, x, first, last)
        if bits:
            extra = exchange(extra, *bits.pop(0))
        a, x, extra = lax.optimization_barrier((a, x, extra))
    inverse = jnp.dot(x.T, x, precision=lax.Precision.HIGHEST)
    return inverse, extra


def body(perturbations, trajectory):
    width = 2 * STEPS
    rows = perturbations.shape[2]
    assert width <= rows
    coeffs = halo(trajectory, width, 3).astype(jnp.float32)
    v = lax.all_to_all(perturbations, "mem", 1, 0, tiled=True)
    members = v.shape[0]
    ncells_all = (
        perturbations.shape[1]
        * perturbations.shape[2]
        * perturbations.shape[3]
        * lax.axis_size("dom")
    )
    hi = lax.Precision.HIGHEST
    flat_v = v.reshape(members, -1)
    gram = jnp.dot(flat_v, flat_v.T, precision=hi)
    pending = butterfly_bits()
    done = []

    def tick(acc, field):
        if pending:
            bit = pending.pop(0)
            acc = exchange(acc, *bit)
            done.append(bit)
        return lax.optimization_barrier((acc, field))

    gram, field = tick(gram, halo(v, width, 2))
    for step in range(STEPS):
        gram, field = tick(gram, forward_step(field, coeffs[step]))
    flat_z = field[:, :, width : width + rows, :].reshape(members, -1)
    cross = jnp.dot(flat_z, flat_z.T, precision=hi)
    both = jnp.stack([gram, cross])
    cross_bits = list(done)
    for step in reversed(range(STEPS)):
        both, field = tick(both, adjoint_step(field, coeffs[step]))
    while pending:
        both = exchange(both, *pending.pop(0))
    gram, cross = both[0], both[1]
    field = field[:, :, width : width + rows, :]
    flat_w = field.reshape(members, -1)
    inverse, cross = invert_beside(gram / ncells_all, cross, cross_bits)
    ritz = jnp.dot(inverse, flat_w, precision=hi)
    for axis, bit in cross_bits:
        cross = exchange(cross, axis, bit)
    projected = cross / ncells_all
    ritz = lax.all_to_all(ritz.reshape(v.shape), "mem", 0, 1, tiled=True)
    return (ritz, projected)


def solution(mesh):
    return jax.shard_map(
        body,
        mesh=mesh,
        in_specs=(P("mem", None, "dom", None), P(None, None, "mem", "dom", None)),
        out_specs=(P("mem", None, "dom", None), P()),
        check_vma=False,
    )
```

```python
import jax
import jax.numpy as jnp
from jax import lax
from jax.experimental import pallas as pl
from jax.experimental.pallas import tpu as pltpu
from jax.sharding import PartitionSpec as P

STEPS = 2


def halo(block, width, dim):
    count = lax.axis_size("dom")
    forward = [(i, i + 1) for i in range(count - 1)]
    backward = [(i + 1, i) for i in range(count - 1)]
    size = block.shape[dim]
    low = lax.ppermute(lax.slice_in_dim(block, size - width, size, axis=dim), "dom", forward)
    high = lax.ppermute(lax.slice_in_dim(block, 0, width, axis=dim), "dom", backward)
    return jnp.concatenate([low, block, high], axis=dim)


def shifted(x, offset, dim):
    pad = [(0, 0)] * x.ndim
    size = x.shape[dim]
    if offset > 0:
        pad[dim] = (0, offset)
        return lax.slice_in_dim(jnp.pad(x, pad), offset, offset + size, axis=dim)
    pad[dim] = (-offset, 0)
    return lax.slice_in_dim(jnp.pad(x, pad), 0, size, axis=dim)


def forward_step(field, coef):
    result = coef[0] * field + coef[1] * shifted(field, -1, 2) + coef[2] * shifted(field, 1, 2)
    return result + coef[3] * shifted(field, -1, 3) + coef[4] * shifted(field, 1, 3)


def adjoint_step(field, coef):
    result = coef[0] * field + shifted(coef[1] * field, 1, 2) + shifted(coef[2] * field, -1, 2)
    return result + shifted(coef[3] * field, 1, 3) + shifted(coef[4] * field, -1, 3)


def butterfly_bits():
    bits = []
    for axis in ("mem", "dom"):
        bit = 1
        while bit < lax.axis_size(axis):
            bits.append((axis, bit))
            bit *= 2
    return bits


def exchange(x, axis, bit):
    count = lax.axis_size(axis)
    return x + lax.ppermute(x, axis, [(i, i ^ bit) for i in range(count)])


def chol_inv_kernel(g_ref, x_ref, a_ref):
    n = g_ref.shape[0]
    a_ref[...] = g_ref[...]
    rows = lax.broadcasted_iota(jnp.int32, (n, n), 0)
    cols = lax.broadcasted_iota(jnp.int32, (n, n), 1)
    x_ref[...] = jnp.where(rows == cols, 1.0, 0.0).astype(jnp.float32)
    lane = lax.broadcasted_iota(jnp.int32, (1, n), 1)
    sub = lax.broadcasted_iota(jnp.int32, (n, 1), 0)

    def step(k, carry):
        a = a_ref[...]
        row = a_ref[pl.ds(k, 1), :]
        pivot = jnp.sum(jnp.where(lane == k, row, 0.0), axis=1, keepdims=True)
        scale = 1.0 / jnp.sqrt(pivot)
        col = jnp.sum(jnp.where(cols == k, a, 0.0), axis=1, keepdims=True)
        below = jnp.where(sub > k, col * scale, 0.0)
        right = jnp.where(lane > k, row * scale, 0.0)
        a_ref[...] = a - below * right
        xrow = x_ref[pl.ds(k, 1), :] * scale
        x_ref[pl.ds(k, 1), :] = xrow
        x_ref[...] = x_ref[...] - below * xrow
        return carry

    lax.fori_loop(0, n, step, 0)


def lower_inverse(gram):
    n = gram.shape[0]
    return pl.pallas_call(
        chol_inv_kernel,
        out_shape=jax.ShapeDtypeStruct((n, n), jnp.float32),
        scratch_shapes=[pltpu.VMEM((n, n), jnp.float32)],
    )(gram)


def invert_beside(gram, extra, bits):
    solved = lower_inverse(gram)
    if bits:
        extra = exchange(extra, *bits.pop(0))
    solved, extra = lax.optimization_barrier((solved, extra))
    inverse = jnp.dot(solved.T, solved, precision=lax.Precision.HIGHEST)
    if bits:
        extra = exchange(extra, *bits.pop(0))
    inverse, extra = lax.optimization_barrier((inverse, extra))
    return inverse, extra


def body(perturbations, trajectory):
    width = 2 * STEPS
    rows = perturbations.shape[2]
    assert width <= rows
    coeffs = halo(trajectory, width, 3).astype(jnp.float32)
    v = lax.all_to_all(perturbations, "mem", 1, 0, tiled=True)
    members = v.shape[0]
    ncells_all = (
        perturbations.shape[1]
        * perturbations.shape[2]
        * perturbations.shape[3]
        * lax.axis_size("dom")
    )
    hi = lax.Precision.HIGHEST
    flat_v = v.reshape(members, -1)
    gram = jnp.dot(flat_v, flat_v.T, precision=hi)
    pending = butterfly_bits()
    done = []

    def tick(acc, field):
        if pending:
            bit = pending.pop(0)
            acc = exchange(acc, *bit)
            done.append(bit)
        return lax.optimization_barrier((acc, field))

    gram, field = tick(gram, halo(v, width, 2))
    for step in range(STEPS):
        gram, field = tick(gram, forward_step(field, coeffs[step]))
    flat_z = field[:, :, width : width + rows, :].reshape(members, -1)
    cross = jnp.dot(flat_z, flat_z.T, precision=hi)
    both = jnp.stack([gram, cross])
    cross_bits = list(done)
    for step in reversed(range(STEPS)):
        both, field = tick(both, adjoint_step(field, coeffs[step]))
    while pending:
        both = exchange(both, *pending.pop(0))
    gram, cross = both[0], both[1]
    field = field[:, :, width : width + rows, :]
    flat_w = field.reshape(members, -1)
    inverse, cross = invert_beside(gram / ncells_all, cross, cross_bits)
    ritz = jnp.dot(inverse, flat_w, precision=hi)
    for axis, bit in cross_bits:
        cross = exchange(cross, axis, bit)
    projected = cross / ncells_all
    ritz = lax.all_to_all(ritz.reshape(v.shape), "mem", 0, 1, tiled=True)
    return (ritz, projected)


def solution(mesh):
    return jax.shard_map(
        body,
        mesh=mesh,
        in_specs=(P("mem", None, "dom", None), P(None, None, "mem", "dom", None)),
        out_specs=(P("mem", None, "dom", None), P()),
        check_vma=False,
    )
```

```python
import jax
import jax.numpy as jnp
from jax import lax
from jax.experimental import pallas as pl
from jax.experimental.pallas import tpu as pltpu
from jax.sharding import PartitionSpec as P

STEPS = 2


def halo(block, width, dim):
    count = lax.axis_size("dom")
    forward = [(i, i + 1) for i in range(count - 1)]
    backward = [(i + 1, i) for i in range(count - 1)]
    size = block.shape[dim]
    low = lax.ppermute(lax.slice_in_dim(block, size - width, size, axis=dim), "dom", forward)
    high = lax.ppermute(lax.slice_in_dim(block, 0, width, axis=dim), "dom", backward)
    return jnp.concatenate([low, block, high], axis=dim)


def shifted(x, offset, dim):
    pad = [(0, 0)] * x.ndim
    size = x.shape[dim]
    if offset > 0:
        pad[dim] = (0, offset)
        return lax.slice_in_dim(jnp.pad(x, pad), offset, offset + size, axis=dim)
    pad[dim] = (-offset, 0)
    return lax.slice_in_dim(jnp.pad(x, pad), 0, size, axis=dim)


def forward_step(field, coef):
    result = coef[0] * field + coef[1] * shifted(field, -1, 2) + coef[2] * shifted(field, 1, 2)
    return result + coef[3] * shifted(field, -1, 3) + coef[4] * shifted(field, 1, 3)


def adjoint_step(field, coef):
    result = coef[0] * field + shifted(coef[1] * field, 1, 2) + shifted(coef[2] * field, -1, 2)
    return result + shifted(coef[3] * field, 1, 3) + shifted(coef[4] * field, -1, 3)


def butterfly_bits():
    bits = []
    for axis in ("mem", "dom"):
        bit = 1
        while bit < lax.axis_size(axis):
            bits.append((axis, bit))
            bit *= 2
    return bits


def exchange(x, axis, bit):
    count = lax.axis_size(axis)
    return x + lax.ppermute(x, axis, [(i, i ^ bit) for i in range(count)])


def chol_inv_kernel(g_ref, x_ref, a_ref):
    n = g_ref.shape[0]
    a_ref[...] = g_ref[...]
    rows = lax.broadcasted_iota(jnp.int32, (n, n), 0)
    cols = lax.broadcasted_iota(jnp.int32, (n, n), 1)
    x_ref[...] = jnp.where(rows == cols, 1.0, 0.0).astype(jnp.float32)
    lane = lax.broadcasted_iota(jnp.int32, (1, n), 1)
    sub = lax.broadcasted_iota(jnp.int32, (n, 1), 0)

    def step(k, carry):
        a = a_ref[...]
        row = a_ref[pl.ds(k, 1), :]
        pivot = jnp.sum(jnp.where(lane == k, row, 0.0), axis=1, keepdims=True)
        scale = 1.0 / jnp.sqrt(pivot)
        col = jnp.sum(jnp.where(cols == k, a, 0.0), axis=1, keepdims=True)
        below = jnp.where(sub > k, col * scale, 0.0)
        right = jnp.where(lane > k, row * scale, 0.0)
        a_ref[...] = a - below * right
        xrow = x_ref[pl.ds(k, 1), :] * scale
        x_ref[pl.ds(k, 1), :] = xrow
        x_ref[...] = x_ref[...] - below * xrow
        return carry

    lax.fori_loop(0, n, step, 0)


def lower_inverse(gram):
    n = gram.shape[0]
    return pl.pallas_call(
        chol_inv_kernel,
        out_shape=jax.ShapeDtypeStruct((n, n), jnp.float32),
        scratch_shapes=[pltpu.VMEM((n, n), jnp.float32)],
    )(gram)


def invert_beside(gram, extra, bits):
    solved = lower_inverse(gram)
    if bits:
        extra = exchange(extra, *bits.pop(0))
    solved, extra = lax.optimization_barrier((solved, extra))
    inverse = jnp.dot(solved.T, solved, precision=lax.Precision.HIGHEST)
    return inverse, extra


def body(perturbations, trajectory):
    width = 2 * STEPS
    rows = perturbations.shape[2]
    assert width <= rows
    coeffs = halo(trajectory, width, 3).astype(jnp.float32)
    v = lax.all_to_all(perturbations, "mem", 1, 0, tiled=True)
    members = v.shape[0]
    ncells_all = (
        perturbations.shape[1]
        * perturbations.shape[2]
        * perturbations.shape[3]
        * lax.axis_size("dom")
    )
    hi = lax.Precision.HIGHEST
    flat_v = v.reshape(members, -1)
    gram = jnp.dot(flat_v, flat_v.T, precision=hi)
    pending = butterfly_bits()
    done = []

    def tick(acc, field):
        if pending:
            bit = pending.pop(0)
            acc = exchange(acc, *bit)
            done.append(bit)
        return lax.optimization_barrier((acc, field))

    field = halo(v, width, 2)
    for step in range(STEPS):
        gram, field = tick(gram, forward_step(field, coeffs[step]))
    flat_z = field[:, :, width : width + rows, :].reshape(members, -1)
    cross = jnp.dot(flat_z, flat_z.T, precision=hi)
    both = jnp.stack([gram, cross])
    cross_bits = list(done)
    for step in reversed(range(STEPS)):
        both, field = tick(both, adjoint_step(field, coeffs[step]))
    while pending:
        both = exchange(both, *pending.pop(0))
    gram, cross = both[0], both[1]
    field = field[:, :, width : width + rows, :]
    flat_w = field.reshape(members, -1)
    inverse, cross = invert_beside(gram / ncells_all, cross, cross_bits)
    ritz = jnp.dot(inverse, flat_w, precision=hi)
    for axis, bit in cross_bits:
        cross = exchange(cross, axis, bit)
    projected = cross / ncells_all
    ritz = lax.all_to_all(ritz.reshape(v.shape), "mem", 0, 1, tiled=True)
    return (ritz, projected)


def solution(mesh):
    return jax.shard_map(
        body,
        mesh=mesh,
        in_specs=(P("mem", None, "dom", None), P(None, None, "mem", "dom", None)),
        out_specs=(P("mem", None, "dom", None), P()),
        check_vma=False,
    )
```

```python
import jax
import jax.numpy as jnp
from jax import lax
from jax.experimental import pallas as pl
from jax.sharding import PartitionSpec as P

STEPS = 2


def halo(block, width, dim):
    count = lax.axis_size("dom")
    forward = [(i, i + 1) for i in range(count - 1)]
    backward = [(i + 1, i) for i in range(count - 1)]
    size = block.shape[dim]
    low = lax.ppermute(lax.slice_in_dim(block, size - width, size, axis=dim), "dom", forward)
    high = lax.ppermute(lax.slice_in_dim(block, 0, width, axis=dim), "dom", backward)
    return jnp.concatenate([low, block, high], axis=dim)


def shifted(x, offset, dim):
    pad = [(0, 0)] * x.ndim
    size = x.shape[dim]
    if offset > 0:
        pad[dim] = (0, offset)
        return lax.slice_in_dim(jnp.pad(x, pad), offset, offset + size, axis=dim)
    pad[dim] = (-offset, 0)
    return lax.slice_in_dim(jnp.pad(x, pad), 0, size, axis=dim)


def forward_step(field, coef):
    result = coef[0] * field + coef[1] * shifted(field, -1, 2) + coef[2] * shifted(field, 1, 2)
    return result + coef[3] * shifted(field, -1, 3) + coef[4] * shifted(field, 1, 3)


def adjoint_step(field, coef):
    result = coef[0] * field + shifted(coef[1] * field, 1, 2) + shifted(coef[2] * field, -1, 2)
    return result + shifted(coef[3] * field, 1, 3) + shifted(coef[4] * field, -1, 3)


def butterfly_bits():
    bits = []
    for axis in ("mem", "dom"):
        bit = 1
        while bit < lax.axis_size(axis):
            bits.append((axis, bit))
            bit *= 2
    return bits


def exchange(x, axis, bit):
    count = lax.axis_size(axis)
    return x + lax.ppermute(x, axis, [(i, i ^ bit) for i in range(count)])


def chol_inv_kernel(g_ref, x_ref):
    n = g_ref.shape[0]
    rows = lax.broadcasted_iota(jnp.int32, (n, n), 0)
    cols = lax.broadcasted_iota(jnp.int32, (n, n), 1)
    lane = lax.broadcasted_iota(jnp.int32, (1, n), 1)
    sub = lax.broadcasted_iota(jnp.int32, (n, 1), 0)

    def step(k, carry):
        a, x = carry
        row = jnp.sum(jnp.where(rows == k, a, 0.0), axis=0, keepdims=True)
        col = jnp.sum(jnp.where(cols == k, a, 0.0), axis=1, keepdims=True)
        pivot = jnp.sum(jnp.where(lane == k, row, 0.0), axis=1, keepdims=True)
        scale = 1.0 / jnp.sqrt(pivot)
        below = jnp.where(sub > k, col * scale, 0.0)
        right = jnp.where(lane > k, row * scale, 0.0)
        a = a - below * right
        xrow = jnp.sum(jnp.where(rows == k, x, 0.0), axis=0, keepdims=True) * scale
        x = jnp.where(rows == k, xrow, x - below * xrow)
        return a, x

    eye = jnp.where(rows == cols, 1.0, 0.0).astype(jnp.float32)
    _, x = lax.fori_loop(0, n, step, (g_ref[...], eye), unroll=4)
    x_ref[...] = x


def lower_inverse(gram):
    n = gram.shape[0]
    return pl.pallas_call(
        chol_inv_kernel,
        out_shape=jax.ShapeDtypeStruct((n, n), jnp.float32),
    )(gram)


def invert_beside(gram, extra, bits):
    solved = lower_inverse(gram)
    if bits:
        extra = exchange(extra, *bits.pop(0))
    solved, extra = lax.optimization_barrier((solved, extra))
    inverse = jnp.dot(solved.T, solved, precision=lax.Precision.HIGHEST)
    return inverse, extra


def body(perturbations, trajectory):
    width = 2 * STEPS
    rows = perturbations.shape[2]
    assert width <= rows
    coeffs = halo(trajectory, width, 3).astype(jnp.float32)
    v = lax.all_to_all(perturbations, "mem", 1, 0, tiled=True)
    members = v.shape[0]
    ncells_all = (
        perturbations.shape[1]
        * perturbations.shape[2]
        * perturbations.shape[3]
        * lax.axis_size("dom")
    )
    hi = lax.Precision.HIGHEST
    flat_v = v.reshape(members, -1)
    gram = jnp.dot(flat_v, flat_v.T, precision=hi)
    pending = butterfly_bits()
    done = []

    def tick(acc, field):
        if pending:
            bit = pending.pop(0)
            acc = exchange(acc, *bit)
            done.append(bit)
        return lax.optimization_barrier((acc, field))

    field = halo(v, width, 2)
    for step in range(STEPS):
        gram, field = tick(gram, forward_step(field, coeffs[step]))
    flat_z = field[:, :, width : width + rows, :].reshape(members, -1)
    cross = jnp.dot(flat_z, flat_z.T, precision=hi)
    both = jnp.stack([gram, cross])
    cross_bits = list(done)
    for step in reversed(range(STEPS)):
        both, field = tick(both, adjoint_step(field, coeffs[step]))
    while pending:
        both = exchange(both, *pending.pop(0))
    gram, cross = both[0], both[1]
    field = field[:, :, width : width + rows, :]
    flat_w = field.reshape(members, -1)
    inverse, cross = invert_beside(gram / ncells_all, cross, cross_bits)
    ritz = jnp.dot(inverse, flat_w, precision=hi)
    for axis, bit in cross_bits:
        cross = exchange(cross, axis, bit)
    projected = cross / ncells_all
    ritz = lax.all_to_all(ritz.reshape(v.shape), "mem", 0, 1, tiled=True)
    return (ritz, projected)


def solution(mesh):
    return jax.shard_map(
        body,
        mesh=mesh,
        in_specs=(P("mem", None, "dom", None), P(None, None, "mem", "dom", None)),
        out_specs=(P("mem", None, "dom", None), P()),
        check_vma=False,
    )
```

```python
import jax
import jax.numpy as jnp
from jax import lax
from jax.experimental import pallas as pl
from jax.experimental.pallas import tpu as pltpu
from jax.sharding import PartitionSpec as P

STEPS = 2


def halo(block, width, dim):
    count = lax.axis_size("dom")
    forward = [(i, i + 1) for i in range(count - 1)]
    backward = [(i + 1, i) for i in range(count - 1)]
    size = block.shape[dim]
    low = lax.ppermute(lax.slice_in_dim(block, size - width, size, axis=dim), "dom", forward)
    high = lax.ppermute(lax.slice_in_dim(block, 0, width, axis=dim), "dom", backward)
    return jnp.concatenate([low, block, high], axis=dim)


def shifted(x, offset, dim):
    pad = [(0, 0)] * x.ndim
    size = x.shape[dim]
    if offset > 0:
        pad[dim] = (0, offset)
        return lax.slice_in_dim(jnp.pad(x, pad), offset, offset + size, axis=dim)
    pad[dim] = (-offset, 0)
    return lax.slice_in_dim(jnp.pad(x, pad), 0, size, axis=dim)


def forward_step(field, coef):
    result = coef[0] * field + coef[1] * shifted(field, -1, 2) + coef[2] * shifted(field, 1, 2)
    return result + coef[3] * shifted(field, -1, 3) + coef[4] * shifted(field, 1, 3)


def adjoint_step(field, coef):
    result = coef[0] * field + shifted(coef[1] * field, 1, 2) + shifted(coef[2] * field, -1, 2)
    return result + shifted(coef[3] * field, 1, 3) + shifted(coef[4] * field, -1, 3)


def butterfly_bits():
    bits = []
    for axis in ("mem", "dom"):
        bit = 1
        while bit < lax.axis_size(axis):
            bits.append((axis, bit))
            bit *= 2
    return bits


def exchange(x, axis, bit):
    count = lax.axis_size(axis)
    return x + lax.ppermute(x, axis, [(i, i ^ bit) for i in range(count)])


def chol_inv_kernel(g_ref, x_ref, a_ref):
    n = g_ref.shape[0]
    a_ref[...] = g_ref[...]
    rows = lax.broadcasted_iota(jnp.int32, (n, n), 0)
    cols = lax.broadcasted_iota(jnp.int32, (n, n), 1)
    x_ref[...] = jnp.where(rows == cols, 1.0, 0.0).astype(jnp.float32)
    lane = lax.broadcasted_iota(jnp.int32, (1, n), 1)
    sub = lax.broadcasted_iota(jnp.int32, (n, 1), 0)

    def step(k, carry):
        a = a_ref[...]
        row = a_ref[pl.ds(k, 1), :]
        pivot = jnp.sum(jnp.where(lane == k, row, 0.0), axis=1, keepdims=True)
        scale = 1.0 / jnp.sqrt(pivot)
        col = jnp.sum(jnp.where(cols == k, a, 0.0), axis=1, keepdims=True)
        below = jnp.where(sub > k, col * scale, 0.0)
        right = jnp.where(lane > k, row * scale, 0.0)
        a_ref[...] = a - below * right
        xrow = x_ref[pl.ds(k, 1), :] * scale
        x_ref[pl.ds(k, 1), :] = xrow
        x_ref[...] = x_ref[...] - below * xrow
        return carry

    lax.fori_loop(0, n, step, 0)


def lower_inverse(gram):
    n = gram.shape[0]
    return pl.pallas_call(
        chol_inv_kernel,
        out_shape=jax.ShapeDtypeStruct((n, n), jnp.float32),
        scratch_shapes=[pltpu.VMEM((n, n), jnp.float32)],
    )(gram)


def invert_beside(gram, extra, bits):
    solved = lower_inverse(gram)
    if bits:
        extra = exchange(extra, *bits.pop(0))
    solved, extra = lax.optimization_barrier((solved, extra))
    inverse = jnp.dot(solved.T, solved, precision=lax.Precision.HIGHEST)
    return inverse, extra


def body(perturbations, trajectory):
    width = 2 * STEPS
    rows = perturbations.shape[2]
    assert width <= rows
    coeffs = halo(trajectory, width, 3).astype(jnp.float32)
    v = lax.all_to_all(perturbations, "mem", 1, 0, tiled=True)
    members = v.shape[0]
    ncells_all = (
        perturbations.shape[1]
        * perturbations.shape[2]
        * perturbations.shape[3]
        * lax.axis_size("dom")
    )
    hi = lax.Precision.HIGHEST
    flat_v = v.reshape(members, -1)
    gram = jnp.dot(flat_v, flat_v.T, precision=hi)
    pending = butterfly_bits()
    done = []

    def tick(acc, field):
        if pending:
            bit = pending.pop(0)
            acc = exchange(acc, *bit)
            done.append(bit)
        return lax.optimization_barrier((acc, field))

    field = halo(v, width, 2)
    for step in range(STEPS):
        gram, field = tick(gram, forward_step(field, coeffs[step]))
    flat_z = field[:, :, width : width + rows, :].reshape(members, -1)
    cross = jnp.dot(flat_z, flat_z.T, precision=hi)
    both = jnp.stack([gram, cross])
    cross_bits = list(done)
    for step in reversed(range(STEPS)):
        field = adjoint_step(field, coeffs[step])
    both, field = tick(both, field)
    while pending:
        both = exchange(both, *pending.pop(0))
    gram, cross = both[0], both[1]
    field = field[:, :, width : width + rows, :]
    flat_w = field.reshape(members, -1)
    inverse, cross = invert_beside(gram / ncells_all, cross, cross_bits)
    ritz = jnp.dot(inverse, flat_w, precision=hi)
    for axis, bit in cross_bits:
        cross = exchange(cross, axis, bit)
    projected = cross / ncells_all
    ritz = lax.all_to_all(ritz.reshape(v.shape), "mem", 0, 1, tiled=True)
    return (ritz, projected)


def solution(mesh):
    return jax.shard_map(
        body,
        mesh=mesh,
        in_specs=(P("mem", None, "dom", None), P(None, None, "mem", "dom", None)),
        out_specs=(P("mem", None, "dom", None), P()),
        check_vma=False,
    )
```

```python
import jax
import jax.numpy as jnp
from jax import lax
from jax.experimental import pallas as pl
from jax.experimental.pallas import tpu as pltpu
from jax.sharding import PartitionSpec as P

STEPS = 2


def halo(block, width, dim):
    count = lax.axis_size("dom")
    forward = [(i, i + 1) for i in range(count - 1)]
    backward = [(i + 1, i) for i in range(count - 1)]
    size = block.shape[dim]
    low = lax.ppermute(lax.slice_in_dim(block, size - width, size, axis=dim), "dom", forward)
    high = lax.ppermute(lax.slice_in_dim(block, 0, width, axis=dim), "dom", backward)
    return jnp.concatenate([low, block, high], axis=dim)


def shifted(x, offset, dim):
    pad = [(0, 0)] * x.ndim
    size = x.shape[dim]
    if offset > 0:
        pad[dim] = (0, offset)
        return lax.slice_in_dim(jnp.pad(x, pad), offset, offset + size, axis=dim)
    pad[dim] = (-offset, 0)
    return lax.slice_in_dim(jnp.pad(x, pad), 0, size, axis=dim)


def forward_step(field, coef):
    result = coef[0] * field + coef[1] * shifted(field, -1, 2) + coef[2] * shifted(field, 1, 2)
    return result + coef[3] * shifted(field, -1, 3) + coef[4] * shifted(field, 1, 3)


def adjoint_step(field, coef):
    result = coef[0] * field + shifted(coef[1] * field, 1, 2) + shifted(coef[2] * field, -1, 2)
    return result + shifted(coef[3] * field, 1, 3) + shifted(coef[4] * field, -1, 3)


def butterfly_bits():
    bits = []
    for axis in ("mem", "dom"):
        bit = 1
        while bit < lax.axis_size(axis):
            bits.append((axis, bit))
            bit *= 2
    return bits


def exchange(x, axis, bit):
    count = lax.axis_size(axis)
    return x + lax.ppermute(x, axis, [(i, i ^ bit) for i in range(count)])


def chol_inv_kernel(g_ref, x_ref, a_ref):
    n = g_ref.shape[0]
    a_ref[...] = g_ref[...]
    rows = lax.broadcasted_iota(jnp.int32, (n, n), 0)
    cols = lax.broadcasted_iota(jnp.int32, (n, n), 1)
    x_ref[...] = jnp.where(rows == cols, 1.0, 0.0).astype(jnp.float32)
    lane = lax.broadcasted_iota(jnp.int32, (1, n), 1)
    sub = lax.broadcasted_iota(jnp.int32, (n, 1), 0)

    def step(k, carry):
        a = a_ref[...]
        row = a_ref[pl.ds(k, 1), :]
        pivot = jnp.sum(jnp.where(lane == k, row, 0.0), axis=1, keepdims=True)
        scale = 1.0 / jnp.sqrt(pivot)
        col = jnp.sum(jnp.where(cols == k, a, 0.0), axis=1, keepdims=True)
        below = jnp.where(sub > k, col * scale, 0.0)
        right = jnp.where(lane > k, row * scale, 0.0)
        a_ref[...] = a - below * right
        xrow = x_ref[pl.ds(k, 1), :] * scale
        x_ref[pl.ds(k, 1), :] = xrow
        x_ref[...] = x_ref[...] - below * xrow
        return carry

    lax.fori_loop(0, n, step, 0)


def lower_inverse(gram):
    n = gram.shape[0]
    return pl.pallas_call(
        chol_inv_kernel,
        out_shape=jax.ShapeDtypeStruct((n, n), jnp.float32),
        scratch_shapes=[pltpu.VMEM((n, n), jnp.float32)],
    )(gram)


def invert_beside(gram, extra, bits):
    solved = lower_inverse(gram)
    if bits:
        extra = exchange(extra, *bits.pop(0))
    solved, extra = lax.optimization_barrier((solved, extra))
    inverse = jnp.dot(solved.T, solved, precision=lax.Precision.HIGHEST)
    return inverse, extra


def body(perturbations, trajectory):
    width = 2 * STEPS
    rows = perturbations.shape[2]
    assert width <= rows
    coeffs = halo(trajectory, width, 3).astype(jnp.float32)
    v = lax.all_to_all(perturbations, "mem", 1, 0, tiled=True)
    members = v.shape[0]
    ncells_all = (
        perturbations.shape[1]
        * perturbations.shape[2]
        * perturbations.shape[3]
        * lax.axis_size("dom")
    )
    hi = lax.Precision.HIGHEST
    gram = jnp.einsum("alij,blij->ab", v, v, precision=hi)
    pending = butterfly_bits()
    done = []

    def tick(acc, field):
        if pending:
            bit = pending.pop(0)
            acc = exchange(acc, *bit)
            done.append(bit)
        return lax.optimization_barrier((acc, field))

    field = halo(v, width, 2)
    for step in range(STEPS):
        gram, field = tick(gram, forward_step(field, coeffs[step]))
    own = field[:, :, width : width + rows, :]
    cross = jnp.einsum("alij,blij->ab", own, own, precision=hi)
    both = jnp.stack([gram, cross])
    cross_bits = list(done)
    for step in reversed(range(STEPS)):
        both, field = tick(both, adjoint_step(field, coeffs[step]))
    while pending:
        both = exchange(both, *pending.pop(0))
    gram, cross = both[0], both[1]
    field = field[:, :, width : width + rows, :]
    inverse, cross = invert_beside(gram / ncells_all, cross, cross_bits)
    ritz = jnp.einsum("ab,blij->alij", inverse, field, precision=hi)
    for axis, bit in cross_bits:
        cross = exchange(cross, axis, bit)
    projected = cross / ncells_all
    ritz = lax.all_to_all(ritz, "mem", 0, 1, tiled=True)
    return (ritz, projected)


def solution(mesh):
    return jax.shard_map(
        body,
        mesh=mesh,
        in_specs=(P("mem", None, "dom", None), P(None, None, "mem", "dom", None)),
        out_specs=(P("mem", None, "dom", None), P()),
        check_vma=False,
    )
```

```python
import jax
import jax.numpy as jnp
from jax import lax
from jax.experimental import pallas as pl
from jax.experimental.pallas import tpu as pltpu
from jax.sharding import PartitionSpec as P

STEPS = 2


def halo(block, width, dim):
    count = lax.axis_size("dom")
    forward = [(i, i + 1) for i in range(count - 1)]
    backward = [(i + 1, i) for i in range(count - 1)]
    size = block.shape[dim]
    low = lax.ppermute(lax.slice_in_dim(block, size - width, size, axis=dim), "dom", forward)
    high = lax.ppermute(lax.slice_in_dim(block, 0, width, axis=dim), "dom", backward)
    return jnp.concatenate([low, block, high], axis=dim)


def shifted(x, offset, dim):
    pad = [(0, 0)] * x.ndim
    size = x.shape[dim]
    if offset > 0:
        pad[dim] = (0, offset)
        return lax.slice_in_dim(jnp.pad(x, pad), offset, offset + size, axis=dim)
    pad[dim] = (-offset, 0)
    return lax.slice_in_dim(jnp.pad(x, pad), 0, size, axis=dim)


def forward_step(field, coef):
    result = coef[0] * field + coef[1] * shifted(field, -1, 2) + coef[2] * shifted(field, 1, 2)
    return result + coef[3] * shifted(field, -1, 3) + coef[4] * shifted(field, 1, 3)


def adjoint_step(field, coef):
    result = coef[0] * field + shifted(coef[1] * field, 1, 2) + shifted(coef[2] * field, -1, 2)
    return result + shifted(coef[3] * field, 1, 3) + shifted(coef[4] * field, -1, 3)


def butterfly_bits():
    bits = []
    for axis in ("mem", "dom"):
        bit = 1
        while bit < lax.axis_size(axis):
            bits.append((axis, bit))
            bit *= 2
    return bits


def exchange(x, axis, bit):
    count = lax.axis_size(axis)
    return x + lax.ppermute(x, axis, [(i, i ^ bit) for i in range(count)])


def chol_inv_kernel(g_ref, x_ref, a_ref):
    n = g_ref.shape[0]
    a_ref[...] = g_ref[...]
    rows = lax.broadcasted_iota(jnp.int32, (n, n), 0)
    cols = lax.broadcasted_iota(jnp.int32, (n, n), 1)
    x_ref[...] = jnp.where(rows == cols, 1.0, 0.0).astype(jnp.float32)
    lane = lax.broadcasted_iota(jnp.int32, (1, n), 1)
    sub = lax.broadcasted_iota(jnp.int32, (n, 1), 0)

    def step(k, carry):
        a = a_ref[...]
        row = a_ref[pl.ds(k, 1), :]
        pivot = jnp.sum(jnp.where(lane == k, row, 0.0), axis=1, keepdims=True)
        scale = 1.0 / jnp.sqrt(pivot)
        col = jnp.sum(jnp.where(cols == k, a, 0.0), axis=1, keepdims=True)
        below = jnp.where(sub > k, col * scale, 0.0)
        right = jnp.where(lane > k, row * scale, 0.0)
        a_ref[...] = a - below * right
        xrow = x_ref[pl.ds(k, 1), :] * scale
        x_ref[pl.ds(k, 1), :] = xrow
        x_ref[...] = x_ref[...] - below * xrow
        return carry

    lax.fori_loop(0, n, step, 0)


def lower_inverse(gram):
    n = gram.shape[0]
    return pl.pallas_call(
        chol_inv_kernel,
        out_shape=jax.ShapeDtypeStruct((n, n), jnp.float32),
        scratch_shapes=[pltpu.VMEM((n, n), jnp.float32)],
    )(gram)


def invert_beside(gram, extra, bits):
    solved = lower_inverse(gram)
    if bits:
        extra = exchange(extra, *bits.pop(0))
    solved, extra = lax.optimization_barrier((solved, extra))
    inverse = jnp.dot(solved.T, solved, precision=lax.Precision.HIGHEST)
    return inverse, extra


def regroup(x, split, concat):
    count = lax.axis_size("mem")
    me = lax.axis_index("mem")
    size = x.shape[split] // count
    pieces = []
    for offset in range(count):
        chunk = lax.dynamic_slice_in_dim(x, ((me + offset) % count) * size, size, split)
        if offset:
            pairs = [(i, (i + offset) % count) for i in range(count)]
            chunk = lax.ppermute(chunk, "mem", pairs)
        pieces.append(chunk)
    order = (me - jnp.arange(count)) % count
    stacked = jnp.take(jnp.stack(pieces), order, axis=0)
    stacked = jnp.moveaxis(stacked, 0, concat)
    shape = list(x.shape)
    shape[split] = size
    shape[concat] *= count
    return stacked.reshape(shape)


def body(perturbations, trajectory):
    width = 2 * STEPS
    rows = perturbations.shape[2]
    assert width <= rows
    coeffs = halo(trajectory, width, 3).astype(jnp.float32)
    v = regroup(perturbations, 1, 0)
    members = v.shape[0]
    ncells_all = (
        perturbations.shape[1]
        * perturbations.shape[2]
        * perturbations.shape[3]
        * lax.axis_size("dom")
    )
    hi = lax.Precision.HIGHEST
    gram = jnp.einsum("alij,blij->ab", v, v, precision=hi)
    pending = butterfly_bits()
    done = []

    def tick(acc, field):
        if pending:
            bit = pending.pop(0)
            acc = exchange(acc, *bit)
            done.append(bit)
        return lax.optimization_barrier((acc, field))

    field = halo(v, width, 2)
    for step in range(STEPS):
        gram, field = tick(gram, forward_step(field, coeffs[step]))
    own = field[:, :, width : width + rows, :]
    cross = jnp.einsum("alij,blij->ab", own, own, precision=hi)
    both = jnp.stack([gram, cross])
    cross_bits = list(done)
    for step in reversed(range(STEPS)):
        both, field = tick(both, adjoint_step(field, coeffs[step]))
    while pending:
        both = exchange(both, *pending.pop(0))
    gram, cross = both[0], both[1]
    field = field[:, :, width : width + rows, :]
    inverse, cross = invert_beside(gram / ncells_all, cross, cross_bits)
    ritz = jnp.einsum("ab,blij->alij", inverse, field, precision=hi)
    for axis, bit in cross_bits:
        cross = exchange(cross, axis, bit)
    projected = cross / ncells_all
    ritz = regroup(ritz, 0, 1)
    return (ritz, projected)


def solution(mesh):
    return jax.shard_map(
        body,
        mesh=mesh,
        in_specs=(P("mem", None, "dom", None), P(None, None, "mem", "dom", None)),
        out_specs=(P("mem", None, "dom", None), P()),
        check_vma=False,
    )
```

```python
import jax
import jax.numpy as jnp
from jax import lax
from jax.experimental import pallas as pl
from jax.experimental.pallas import tpu as pltpu
from jax.sharding import PartitionSpec as P

STEPS = 2


def halo(block, width, dim):
    count = lax.axis_size("dom")
    forward = [(i, i + 1) for i in range(count - 1)]
    backward = [(i + 1, i) for i in range(count - 1)]
    size = block.shape[dim]
    low = lax.ppermute(lax.slice_in_dim(block, size - width, size, axis=dim), "dom", forward)
    high = lax.ppermute(lax.slice_in_dim(block, 0, width, axis=dim), "dom", backward)
    return jnp.concatenate([low, block, high], axis=dim)


def shifted(x, offset, dim):
    pad = [(0, 0)] * x.ndim
    size = x.shape[dim]
    if offset > 0:
        pad[dim] = (0, offset)
        return lax.slice_in_dim(jnp.pad(x, pad), offset, offset + size, axis=dim)
    pad[dim] = (-offset, 0)
    return lax.slice_in_dim(jnp.pad(x, pad), 0, size, axis=dim)


def forward_step(field, coef):
    result = coef[0] * field + coef[1] * shifted(field, -1, 2) + coef[2] * shifted(field, 1, 2)
    return result + coef[3] * shifted(field, -1, 3) + coef[4] * shifted(field, 1, 3)


def adjoint_step(field, coef):
    result = coef[0] * field + shifted(coef[1] * field, 1, 2) + shifted(coef[2] * field, -1, 2)
    return result + shifted(coef[3] * field, 1, 3) + shifted(coef[4] * field, -1, 3)


def butterfly_bits():
    bits = []
    for axis in ("mem", "dom"):
        bit = 1
        while bit < lax.axis_size(axis):
            bits.append((axis, bit))
            bit *= 2
    return bits


def exchange(x, axis, bit):
    count = lax.axis_size(axis)
    return x + lax.ppermute(x, axis, [(i, i ^ bit) for i in range(count)])


def chol_inv_kernel(g_ref, x_ref, a_ref):
    n = g_ref.shape[0]
    a_ref[...] = g_ref[...]
    rows = lax.broadcasted_iota(jnp.int32, (n, n), 0)
    cols = lax.broadcasted_iota(jnp.int32, (n, n), 1)
    x_ref[...] = jnp.where(rows == cols, 1.0, 0.0).astype(jnp.float32)
    lane = lax.broadcasted_iota(jnp.int32, (1, n), 1)
    sub = lax.broadcasted_iota(jnp.int32, (n, 1), 0)

    def step(k, carry):
        a = a_ref[...]
        row = a_ref[pl.ds(k, 1), :]
        pivot = jnp.sum(jnp.where(lane == k, row, 0.0), axis=1, keepdims=True)
        scale = 1.0 / jnp.sqrt(pivot)
        col = jnp.sum(jnp.where(cols == k, a, 0.0), axis=1, keepdims=True)
        below = jnp.where(sub > k, col * scale, 0.0)
        right = jnp.where(lane > k, row * scale, 0.0)
        a_ref[...] = a - below * right
        xrow = x_ref[pl.ds(k, 1), :] * scale
        x_ref[pl.ds(k, 1), :] = xrow
        x_ref[...] = x_ref[...] - below * xrow
        return carry

    lax.fori_loop(0, n, step, 0)


def lower_inverse(gram):
    n = gram.shape[0]
    return pl.pallas_call(
        chol_inv_kernel,
        out_shape=jax.ShapeDtypeStruct((n, n), jnp.float32),
        scratch_shapes=[pltpu.VMEM((n, n), jnp.float32)],
    )(gram)


def invert_beside(gram, extra, bits):
    solved = lower_inverse(gram)
    if bits:
        extra = exchange(extra, *bits.pop(0))
    solved, extra = lax.optimization_barrier((solved, extra))
    inverse = jnp.dot(solved.T, solved, precision=lax.Precision.HIGHEST)
    return inverse, extra


def body(perturbations, trajectory):
    width = 2 * STEPS
    rows = perturbations.shape[2]
    assert width <= rows
    coeffs = halo(trajectory, width, 3).astype(jnp.float32)
    v = lax.all_to_all(perturbations, "mem", 1, 0, tiled=True)
    members = v.shape[0]
    ncells_all = (
        perturbations.shape[1]
        * perturbations.shape[2]
        * perturbations.shape[3]
        * lax.axis_size("dom")
    )
    hi = lax.Precision.HIGHEST
    flat_v = v.reshape(members, -1)
    gram = jnp.dot(flat_v, flat_v.T, precision=hi)
    pending = butterfly_bits()
    done = []

    def tick(acc, field):
        if pending:
            bit = pending.pop(0)
            acc = exchange(acc, *bit)
            done.append(bit)
        return lax.optimization_barrier((acc, field))

    field = halo(v, width, 2)
    for step in range(STEPS):
        field = forward_step(field, coeffs[step])
    flat_z = field[:, :, width : width + rows, :].reshape(members, -1)
    cross = jnp.dot(flat_z, flat_z.T, precision=hi)
    both = jnp.stack([gram, cross])
    cross_bits = list(done)
    for step in reversed(range(STEPS)):
        both, field = tick(both, adjoint_step(field, coeffs[step]))
    while pending:
        both = exchange(both, *pending.pop(0))
    gram, cross = both[0], both[1]
    field = field[:, :, width : width + rows, :]
    flat_w = field.reshape(members, -1)
    inverse, cross = invert_beside(gram / ncells_all, cross, cross_bits)
    ritz = jnp.dot(inverse, flat_w, precision=hi)
    for axis, bit in cross_bits:
        cross = exchange(cross, axis, bit)
    projected = cross / ncells_all
    ritz = lax.all_to_all(ritz.reshape(v.shape), "mem", 0, 1, tiled=True)
    return (ritz, projected)


def solution(mesh):
    return jax.shard_map(
        body,
        mesh=mesh,
        in_specs=(P("mem", None, "dom", None), P(None, None, "mem", "dom", None)),
        out_specs=(P("mem", None, "dom", None), P()),
        check_vma=False,
    )
```

```python
import jax
import jax.numpy as jnp
from jax import lax
from jax.experimental import pallas as pl
from jax.experimental.pallas import tpu as pltpu
from jax.sharding import PartitionSpec as P

STEPS = 2


def halo(block, width, dim):
    count = lax.axis_size("dom")
    forward = [(i, i + 1) for i in range(count - 1)]
    backward = [(i + 1, i) for i in range(count - 1)]
    size = block.shape[dim]
    low = lax.ppermute(lax.slice_in_dim(block, size - width, size, axis=dim), "dom", forward)
    high = lax.ppermute(lax.slice_in_dim(block, 0, width, axis=dim), "dom", backward)
    return jnp.concatenate([low, block, high], axis=dim)


def shifted(x, offset, dim):
    pad = [(0, 0)] * x.ndim
    size = x.shape[dim]
    if offset > 0:
        pad[dim] = (0, offset)
        return lax.slice_in_dim(jnp.pad(x, pad), offset, offset + size, axis=dim)
    pad[dim] = (-offset, 0)
    return lax.slice_in_dim(jnp.pad(x, pad), 0, size, axis=dim)


def forward_step(field, coef):
    result = coef[0] * field + coef[1] * shifted(field, -1, 2) + coef[2] * shifted(field, 1, 2)
    return result + coef[3] * shifted(field, -1, 3) + coef[4] * shifted(field, 1, 3)


def adjoint_step(field, coef):
    result = coef[0] * field + shifted(coef[1] * field, 1, 2) + shifted(coef[2] * field, -1, 2)
    return result + shifted(coef[3] * field, 1, 3) + shifted(coef[4] * field, -1, 3)


def butterfly_bits():
    bits = []
    for axis in ("mem", "dom"):
        bit = 1
        while bit < lax.axis_size(axis):
            bits.append((axis, bit))
            bit *= 2
    return bits


def exchange(x, axis, bit):
    count = lax.axis_size(axis)
    return x + lax.ppermute(x, axis, [(i, i ^ bit) for i in range(count)])


def chol_inv_kernel(g_ref, x_ref, a_ref):
    n = g_ref.shape[0]
    a_ref[...] = g_ref[...]
    rows = lax.broadcasted_iota(jnp.int32, (n, n), 0)
    cols = lax.broadcasted_iota(jnp.int32, (n, n), 1)
    x_ref[...] = jnp.where(rows == cols, 1.0, 0.0).astype(jnp.float32)
    lane = lax.broadcasted_iota(jnp.int32, (1, n), 1)
    sub = lax.broadcasted_iota(jnp.int32, (n, 1), 0)

    def pick(vec, index):
        return jnp.sum(jnp.where(lane == index, vec, 0.0), axis=1, keepdims=True)

    def step(half, carry):
        k = 2 * half
        a = a_ref[...]
        row0 = a_ref[pl.ds(k, 1), :]
        row1 = a_ref[pl.ds(k + 1, 1), :]
        col0 = jnp.sum(jnp.where(cols == k, a, 0.0), axis=1, keepdims=True)
        col1 = jnp.sum(jnp.where(cols == k + 1, a, 0.0), axis=1, keepdims=True)
        scale0 = 1.0 / jnp.sqrt(pick(row0, k))
        below0 = jnp.where(sub > k, col0 * scale0, 0.0)
        right0 = jnp.where(lane > k, row0 * scale0, 0.0)
        link = pick(right0, k + 1)
        row1 = row1 - link * right0
        col1 = col1 - below0 * link
        scale1 = 1.0 / jnp.sqrt(pick(row1, k + 1))
        below1 = jnp.where(sub > k + 1, col1 * scale1, 0.0)
        right1 = jnp.where(lane > k + 1, row1 * scale1, 0.0)
        a_ref[...] = a - below0 * right0 - below1 * right1
        x = x_ref[...]
        xrow0 = x_ref[pl.ds(k, 1), :] * scale0
        xrow1 = (x_ref[pl.ds(k + 1, 1), :] - link * xrow0) * scale1
        x = x - below0 * xrow0 - below1 * xrow1
        x = jnp.where(rows == k, xrow0, jnp.where(rows == k + 1, xrow1, x))
        x_ref[...] = x
        return carry

    lax.fori_loop(0, n // 2, step, 0)


def lower_inverse(gram):
    n = gram.shape[0]
    assert n % 2 == 0
    return pl.pallas_call(
        chol_inv_kernel,
        out_shape=jax.ShapeDtypeStruct((n, n), jnp.float32),
        scratch_shapes=[pltpu.VMEM((n, n), jnp.float32)],
    )(gram)


def invert_beside(gram, extra, bits):
    solved = lower_inverse(gram)
    if bits:
        extra = exchange(extra, *bits.pop(0))
    solved, extra = lax.optimization_barrier((solved, extra))
    inverse = jnp.dot(solved.T, solved, precision=lax.Precision.HIGHEST)
    return inverse, extra


def body(perturbations, trajectory):
    width = 2 * STEPS
    rows = perturbations.shape[2]
    assert width <= rows
    coeffs = halo(trajectory, width, 3).astype(jnp.float32)
    v = lax.all_to_all(perturbations, "mem", 1, 0, tiled=True)
    members = v.shape[0]
    ncells_all = (
        perturbations.shape[1]
        * perturbations.shape[2]
        * perturbations.shape[3]
        * lax.axis_size("dom")
    )
    hi = lax.Precision.HIGHEST
    flat_v = v.reshape(members, -1)
    gram = jnp.dot(flat_v, flat_v.T, precision=hi)
    pending = butterfly_bits()
    done = []

    def tick(acc, field):
        if pending:
            bit = pending.pop(0)
            acc = exchange(acc, *bit)
            done.append(bit)
        return lax.optimization_barrier((acc, field))

    field = halo(v, width, 2)
    for step in range(STEPS):
        gram, field = tick(gram, forward_step(field, coeffs[step]))
    flat_z = field[:, :, width : width + rows, :].reshape(members, -1)
    cross = jnp.dot(flat_z, flat_z.T, precision=hi)
    both = jnp.stack([gram, cross])
    cross_bits = list(done)
    for step in reversed(range(STEPS)):
        both, field = tick(both, adjoint_step(field, coeffs[step]))
    while pending:
        both = exchange(both, *pending.pop(0))
    gram, cross = both[0], both[1]
    field = field[:, :, width : width + rows, :]
    flat_w = field.reshape(members, -1)
    inverse, cross = invert_beside(gram / ncells_all, cross, cross_bits)
    ritz = jnp.dot(inverse, flat_w, precision=hi)
    for axis, bit in cross_bits:
        cross = exchange(cross, axis, bit)
    projected = cross / ncells_all
    ritz = lax.all_to_all(ritz.reshape(v.shape), "mem", 0, 1, tiled=True)
    return (ritz, projected)


def solution(mesh):
    return jax.shard_map(
        body,
        mesh=mesh,
        in_specs=(P("mem", None, "dom", None), P(None, None, "mem", "dom", None)),
        out_specs=(P("mem", None, "dom", None), P()),
        check_vma=False,
    )
```

```python
import jax
import jax.numpy as jnp
from jax import lax
from jax.experimental import pallas as pl
from jax.experimental.pallas import tpu as pltpu
from jax.sharding import PartitionSpec as P

STEPS = 2


def halo(block, width, dim):
    count = lax.axis_size("dom")
    forward = [(i, i + 1) for i in range(count - 1)]
    backward = [(i + 1, i) for i in range(count - 1)]
    size = block.shape[dim]
    low = lax.ppermute(lax.slice_in_dim(block, size - width, size, axis=dim), "dom", forward)
    high = lax.ppermute(lax.slice_in_dim(block, 0, width, axis=dim), "dom", backward)
    return jnp.concatenate([low, block, high], axis=dim)


def shifted(x, offset, dim):
    pad = [(0, 0)] * x.ndim
    size = x.shape[dim]
    if offset > 0:
        pad[dim] = (0, offset)
        return lax.slice_in_dim(jnp.pad(x, pad), offset, offset + size, axis=dim)
    pad[dim] = (-offset, 0)
    return lax.slice_in_dim(jnp.pad(x, pad), 0, size, axis=dim)


def forward_step(field, coef):
    result = coef[0] * field + coef[1] * shifted(field, -1, 2) + coef[2] * shifted(field, 1, 2)
    return result + coef[3] * shifted(field, -1, 3) + coef[4] * shifted(field, 1, 3)


def adjoint_step(field, coef):
    result = coef[0] * field + shifted(coef[1] * field, 1, 2) + shifted(coef[2] * field, -1, 2)
    return result + shifted(coef[3] * field, 1, 3) + shifted(coef[4] * field, -1, 3)


def butterfly_bits():
    bits = []
    for axis in ("mem", "dom"):
        bit = 1
        while bit < lax.axis_size(axis):
            bits.append((axis, bit))
            bit *= 2
    return bits


def exchange(x, axis, bit):
    count = lax.axis_size(axis)
    return x + lax.ppermute(x, axis, [(i, i ^ bit) for i in range(count)])


def chol_inv_kernel(g_ref, x_ref, a_ref):
    n = g_ref.shape[0]
    a_ref[...] = g_ref[...]
    rows = lax.broadcasted_iota(jnp.int32, (n, n), 0)
    cols = lax.broadcasted_iota(jnp.int32, (n, n), 1)
    x_ref[...] = jnp.where(rows == cols, 1.0, 0.0).astype(jnp.float32)
    lane = lax.broadcasted_iota(jnp.int32, (1, n), 1)
    sub = lax.broadcasted_iota(jnp.int32, (n, 1), 0)

    def step(k, carry):
        a = a_ref[...]
        row = a_ref[pl.ds(k, 1), :]
        pivot = jnp.sum(jnp.where(lane == k, row, 0.0), axis=1, keepdims=True)
        scale = 1.0 / jnp.sqrt(pivot)
        col = jnp.transpose(row)
        below = jnp.where(sub > k, col * scale, 0.0)
        right = jnp.where(lane > k, row * scale, 0.0)
        a_ref[...] = a - below * right
        xrow = x_ref[pl.ds(k, 1), :] * scale
        x_ref[pl.ds(k, 1), :] = xrow
        x_ref[...] = x_ref[...] - below * xrow
        return carry

    lax.fori_loop(0, n, step, 0)


def lower_inverse(gram):
    n = gram.shape[0]
    return pl.pallas_call(
        chol_inv_kernel,
        out_shape=jax.ShapeDtypeStruct((n, n), jnp.float32),
        scratch_shapes=[pltpu.VMEM((n, n), jnp.float32)],
    )(gram)


def invert_beside(gram, extra, bits):
    solved = lower_inverse(gram)
    if bits:
        extra = exchange(extra, *bits.pop(0))
    solved, extra = lax.optimization_barrier((solved, extra))
    inverse = jnp.dot(solved.T, solved, precision=lax.Precision.HIGHEST)
    return inverse, extra


def body(perturbations, trajectory):
    width = 2 * STEPS
    rows = perturbations.shape[2]
    assert width <= rows
    coeffs = halo(trajectory, width, 3).astype(jnp.float32)
    v = lax.all_to_all(perturbations, "mem", 1, 0, tiled=True)
    members = v.shape[0]
    ncells_all = (
        perturbations.shape[1]
        * perturbations.shape[2]
        * perturbations.shape[3]
        * lax.axis_size("dom")
    )
    hi = lax.Precision.HIGHEST
    flat_v = v.reshape(members, -1)
    gram = jnp.dot(flat_v, flat_v.T, precision=hi)
    pending = butterfly_bits()
    done = []

    def tick(acc, field):
        if pending:
            bit = pending.pop(0)
            acc = exchange(acc, *bit)
            done.append(bit)
        return lax.optimization_barrier((acc, field))

    field = halo(v, width, 2)
    for step in range(STEPS):
        gram, field = tick(gram, forward_step(field, coeffs[step]))
    flat_z = field[:, :, width : width + rows, :].reshape(members, -1)
    cross = jnp.dot(flat_z, flat_z.T, precision=hi)
    both = jnp.stack([gram, cross])
    cross_bits = list(done)
    for step in reversed(range(STEPS)):
        both, field = tick(both, adjoint_step(field, coeffs[step]))
    while pending:
        both = exchange(both, *pending.pop(0))
    gram, cross = both[0], both[1]
    field = field[:, :, width : width + rows, :]
    flat_w = field.reshape(members, -1)
    inverse, cross = invert_beside(gram / ncells_all, cross, cross_bits)
    ritz = jnp.dot(inverse, flat_w, precision=hi)
    for axis, bit in cross_bits:
        cross = exchange(cross, axis, bit)
    projected = cross / ncells_all
    ritz = lax.all_to_all(ritz.reshape(v.shape), "mem", 0, 1, tiled=True)
    return (ritz, projected)


def solution(mesh):
    return jax.shard_map(
        body,
        mesh=mesh,
        in_specs=(P("mem", None, "dom", None), P(None, None, "mem", "dom", None)),
        out_specs=(P("mem", None, "dom", None), P()),
        check_vma=False,
    )
```

```python
import jax
import jax.numpy as jnp
from jax import lax
from jax.experimental import pallas as pl
from jax.experimental.pallas import tpu as pltpu
from jax.sharding import PartitionSpec as P

STEPS = 2


def halo(block, width, dim):
    count = lax.axis_size("dom")
    forward = [(i, i + 1) for i in range(count - 1)]
    backward = [(i + 1, i) for i in range(count - 1)]
    size = block.shape[dim]
    low = lax.ppermute(lax.slice_in_dim(block, size - width, size, axis=dim), "dom", forward)
    high = lax.ppermute(lax.slice_in_dim(block, 0, width, axis=dim), "dom", backward)
    return jnp.concatenate([low, block, high], axis=dim)


def shifted(x, offset, dim):
    pad = [(0, 0)] * x.ndim
    size = x.shape[dim]
    if offset > 0:
        pad[dim] = (0, offset)
        return lax.slice_in_dim(jnp.pad(x, pad), offset, offset + size, axis=dim)
    pad[dim] = (-offset, 0)
    return lax.slice_in_dim(jnp.pad(x, pad), 0, size, axis=dim)


def forward_step(field, coef):
    result = coef[0] * field + coef[1] * shifted(field, -1, 2) + coef[2] * shifted(field, 1, 2)
    return result + coef[3] * shifted(field, -1, 3) + coef[4] * shifted(field, 1, 3)


def adjoint_step(field, coef):
    result = coef[0] * field + shifted(coef[1] * field, 1, 2) + shifted(coef[2] * field, -1, 2)
    return result + shifted(coef[3] * field, 1, 3) + shifted(coef[4] * field, -1, 3)


def butterfly_bits():
    bits = []
    for axis in ("mem", "dom"):
        bit = 1
        while bit < lax.axis_size(axis):
            bits.append((axis, bit))
            bit *= 2
    return bits


def exchange(x, axis, bit):
    count = lax.axis_size(axis)
    return x + lax.ppermute(x, axis, [(i, i ^ bit) for i in range(count)])


def chol_inv_kernel(g_ref, x_ref, a_ref):
    n = g_ref.shape[0]
    a_ref[...] = g_ref[...]
    rows = lax.broadcasted_iota(jnp.int32, (n, n), 0)
    cols = lax.broadcasted_iota(jnp.int32, (n, n), 1)
    x_ref[...] = jnp.where(rows == cols, 1.0, 0.0).astype(jnp.float32)
    lane = lax.broadcasted_iota(jnp.int32, (1, n), 1)
    sub = lax.broadcasted_iota(jnp.int32, (n, 1), 0)

    def step(k, carry):
        a = a_ref[...]
        row = a_ref[pl.ds(k, 1), :]
        pivot = jnp.sum(jnp.where(lane == k, row, 0.0), axis=1, keepdims=True)
        scale = 1.0 / jnp.sqrt(pivot)
        col = jnp.sum(jnp.where(cols == k, a, 0.0), axis=1, keepdims=True)
        below = jnp.where(sub > k, col * scale, 0.0)
        right = jnp.where(lane > k, row * scale, 0.0)
        a_ref[...] = a - below * right
        xrow = x_ref[pl.ds(k, 1), :] * scale
        x_ref[pl.ds(k, 1), :] = xrow
        x_ref[...] = x_ref[...] - below * xrow
        return carry

    lax.fori_loop(0, n, step, 0)


def inverse_kernel(g_ref, o_ref, x_ref, a_ref):
    chol_inv_kernel(g_ref, x_ref, a_ref)
    x = x_ref[...]
    o_ref[...] = lax.dot_general(
        x, x, (((0,), (0,)), ((), ())), precision=lax.Precision.HIGHEST,
        preferred_element_type=jnp.float32,
    )


def invert_beside(gram, extra, bits):
    n = gram.shape[0]
    inverse = pl.pallas_call(
        inverse_kernel,
        out_shape=jax.ShapeDtypeStruct((n, n), jnp.float32),
        scratch_shapes=[pltpu.VMEM((n, n), jnp.float32), pltpu.VMEM((n, n), jnp.float32)],
    )(gram)
    if bits:
        extra = exchange(extra, *bits.pop(0))
    inverse, extra = lax.optimization_barrier((inverse, extra))
    return inverse, extra


def body(perturbations, trajectory):
    width = 2 * STEPS
    rows = perturbations.shape[2]
    assert width <= rows
    coeffs = halo(trajectory, width, 3).astype(jnp.float32)
    v = lax.all_to_all(perturbations, "mem", 1, 0, tiled=True)
    members = v.shape[0]
    ncells_all = (
        perturbations.shape[1]
        * perturbations.shape[2]
        * perturbations.shape[3]
        * lax.axis_size("dom")
    )
    hi = lax.Precision.HIGHEST
    flat_v = v.reshape(members, -1)
    gram = jnp.dot(flat_v, flat_v.T, precision=hi)
    pending = butterfly_bits()
    done = []

    def tick(acc, field):
        if pending:
            bit = pending.pop(0)
            acc = exchange(acc, *bit)
            done.append(bit)
        return lax.optimization_barrier((acc, field))

    field = halo(v, width, 2)
    for step in range(STEPS):
        gram, field = tick(gram, forward_step(field, coeffs[step]))
    flat_z = field[:, :, width : width + rows, :].reshape(members, -1)
    cross = jnp.dot(flat_z, flat_z.T, precision=hi)
    both = jnp.stack([gram, cross])
    cross_bits = list(done)
    for step in reversed(range(STEPS)):
        both, field = tick(both, adjoint_step(field, coeffs[step]))
    while pending:
        both = exchange(both, *pending.pop(0))
    gram, cross = both[0], both[1]
    field = field[:, :, width : width + rows, :]
    flat_w = field.reshape(members, -1)
    inverse, cross = invert_beside(gram / ncells_all, cross, cross_bits)
    ritz = jnp.dot(inverse, flat_w, precision=hi)
    for axis, bit in cross_bits:
        cross = exchange(cross, axis, bit)
    projected = cross / ncells_all
    ritz = lax.all_to_all(ritz.reshape(v.shape), "mem", 0, 1, tiled=True)
    return (ritz, projected)


def solution(mesh):
    return jax.shard_map(
        body,
        mesh=mesh,
        in_specs=(P("mem", None, "dom", None), P(None, None, "mem", "dom", None)),
        out_specs=(P("mem", None, "dom", None), P()),
        check_vma=False,
    )
```

```python
import jax
import jax.numpy as jnp
from jax import lax
from jax.experimental import pallas as pl
from jax.experimental.pallas import tpu as pltpu
from jax.sharding import PartitionSpec as P

STEPS = 2


def halo(block, width, dim):
    count = lax.axis_size("dom")
    forward = [(i, i + 1) for i in range(count - 1)]
    backward = [(i + 1, i) for i in range(count - 1)]
    size = block.shape[dim]
    low = lax.ppermute(lax.slice_in_dim(block, size - width, size, axis=dim), "dom", forward)
    high = lax.ppermute(lax.slice_in_dim(block, 0, width, axis=dim), "dom", backward)
    return jnp.concatenate([low, block, high], axis=dim)


def shifted(x, offset, dim):
    pad = [(0, 0)] * x.ndim
    size = x.shape[dim]
    if offset > 0:
        pad[dim] = (0, offset)
        return lax.slice_in_dim(jnp.pad(x, pad), offset, offset + size, axis=dim)
    pad[dim] = (-offset, 0)
    return lax.slice_in_dim(jnp.pad(x, pad), 0, size, axis=dim)


def forward_step(field, coef):
    result = coef[0] * field + coef[1] * shifted(field, -1, 2) + coef[2] * shifted(field, 1, 2)
    return result + coef[3] * shifted(field, -1, 3) + coef[4] * shifted(field, 1, 3)


def adjoint_step(field, coef):
    result = coef[0] * field + shifted(coef[1] * field, 1, 2) + shifted(coef[2] * field, -1, 2)
    return result + shifted(coef[3] * field, 1, 3) + shifted(coef[4] * field, -1, 3)


def butterfly_bits():
    rings = {"mem": (2,), "dom": (4,)}
    bits = []
    for axis in ("mem", "dom"):
        bit = 1
        while bit < lax.axis_size(axis):
            mask = bit | (bit // 2) if bit in rings[axis] else bit
            bits.append((axis, mask))
            bit *= 2
    return bits


def exchange(x, axis, bit):
    count = lax.axis_size(axis)
    return x + lax.ppermute(x, axis, [(i, i ^ bit) for i in range(count)])


def chol_inv_kernel(g_ref, x_ref, a_ref):
    n = g_ref.shape[0]
    a_ref[...] = g_ref[...]
    rows = lax.broadcasted_iota(jnp.int32, (n, n), 0)
    cols = lax.broadcasted_iota(jnp.int32, (n, n), 1)
    x_ref[...] = jnp.where(rows == cols, 1.0, 0.0).astype(jnp.float32)
    lane = lax.broadcasted_iota(jnp.int32, (1, n), 1)
    sub = lax.broadcasted_iota(jnp.int32, (n, 1), 0)

    def step(k, carry):
        a = a_ref[...]
        row = a_ref[pl.ds(k, 1), :]
        pivot = jnp.sum(jnp.where(lane == k, row, 0.0), axis=1, keepdims=True)
        scale = 1.0 / jnp.sqrt(pivot)
        col = jnp.sum(jnp.where(cols == k, a, 0.0), axis=1, keepdims=True)
        below = jnp.where(sub > k, col * scale, 0.0)
        right = jnp.where(lane > k, row * scale, 0.0)
        a_ref[...] = a - below * right
        xrow = x_ref[pl.ds(k, 1), :] * scale
        x_ref[pl.ds(k, 1), :] = xrow
        x_ref[...] = x_ref[...] - below * xrow
        return carry

    lax.fori_loop(0, n, step, 0)


def lower_inverse(gram):
    n = gram.shape[0]
    return pl.pallas_call(
        chol_inv_kernel,
        out_shape=jax.ShapeDtypeStruct((n, n), jnp.float32),
        scratch_shapes=[pltpu.VMEM((n, n), jnp.float32)],
    )(gram)


def invert_beside(gram, extra, bits):
    solved = lower_inverse(gram)
    if bits:
        extra = exchange(extra, *bits.pop(0))
    solved, extra = lax.optimization_barrier((solved, extra))
    inverse = jnp.dot(solved.T, solved, precision=lax.Precision.HIGHEST)
    return inverse, extra


def body(perturbations, trajectory):
    width = 2 * STEPS
    rows = perturbations.shape[2]
    assert width <= rows
    coeffs = halo(trajectory, width, 3).astype(jnp.float32)
    v = lax.all_to_all(perturbations, "mem", 1, 0, tiled=True)
    members = v.shape[0]
    ncells_all = (
        perturbations.shape[1]
        * perturbations.shape[2]
        * perturbations.shape[3]
        * lax.axis_size("dom")
    )
    hi = lax.Precision.HIGHEST
    flat_v = v.reshape(members, -1)
    gram = jnp.dot(flat_v, flat_v.T, precision=hi)
    pending = butterfly_bits()
    done = []

    def tick(acc, field):
        if pending:
            bit = pending.pop(0)
            acc = exchange(acc, *bit)
            done.append(bit)
        return lax.optimization_barrier((acc, field))

    field = halo(v, width, 2)
    for step in range(STEPS):
        gram, field = tick(gram, forward_step(field, coeffs[step]))
    flat_z = field[:, :, width : width + rows, :].reshape(members, -1)
    cross = jnp.dot(flat_z, flat_z.T, precision=hi)
    both = jnp.stack([gram, cross])
    cross_bits = list(done)
    for step in reversed(range(STEPS)):
        both, field = tick(both, adjoint_step(field, coeffs[step]))
    while pending:
        both = exchange(both, *pending.pop(0))
    gram, cross = both[0], both[1]
    field = field[:, :, width : width + rows, :]
    flat_w = field.reshape(members, -1)
    inverse, cross = invert_beside(gram / ncells_all, cross, cross_bits)
    ritz = jnp.dot(inverse, flat_w, precision=hi)
    for axis, bit in cross_bits:
        cross = exchange(cross, axis, bit)
    projected = cross / ncells_all
    ritz = lax.all_to_all(ritz.reshape(v.shape), "mem", 0, 1, tiled=True)
    return (ritz, projected)


def solution(mesh):
    return jax.shard_map(
        body,
        mesh=mesh,
        in_specs=(P("mem", None, "dom", None), P(None, None, "mem", "dom", None)),
        out_specs=(P("mem", None, "dom", None), P()),
        check_vma=False,
    )
```

```python
import jax
import jax.numpy as jnp
from jax import lax
from jax.experimental import pallas as pl
from jax.experimental.pallas import tpu as pltpu
from jax.sharding import PartitionSpec as P

STEPS = 2


def halo(block, width, dim):
    count = lax.axis_size("dom")
    forward = [(i, i + 1) for i in range(count - 1)]
    backward = [(i + 1, i) for i in range(count - 1)]
    size = block.shape[dim]
    low = lax.ppermute(lax.slice_in_dim(block, size - width, size, axis=dim), "dom", forward)
    high = lax.ppermute(lax.slice_in_dim(block, 0, width, axis=dim), "dom", backward)
    return jnp.concatenate([low, block, high], axis=dim)


def shifted(x, offset, dim):
    pad = [(0, 0)] * x.ndim
    size = x.shape[dim]
    if offset > 0:
        pad[dim] = (0, offset)
        return lax.slice_in_dim(jnp.pad(x, pad), offset, offset + size, axis=dim)
    pad[dim] = (-offset, 0)
    return lax.slice_in_dim(jnp.pad(x, pad), 0, size, axis=dim)


def forward_step(field, coef):
    result = coef[0] * field + coef[1] * shifted(field, -1, 2) + coef[2] * shifted(field, 1, 2)
    return result + coef[3] * shifted(field, -1, 3) + coef[4] * shifted(field, 1, 3)


def adjoint_step(field, coef):
    result = coef[0] * field + shifted(coef[1] * field, 1, 2) + shifted(coef[2] * field, -1, 2)
    return result + shifted(coef[3] * field, 1, 3) + shifted(coef[4] * field, -1, 3)


def butterfly_bits():
    rings = {"mem": (2,), "dom": (4,)}
    bits = []
    for axis in ("mem", "dom"):
        bit = 1
        while bit < lax.axis_size(axis):
            mask = bit | (bit // 2) if bit in rings[axis] else bit
            bits.append((axis, mask))
            bit *= 2
    return bits


def exchange(x, axis, bit):
    count = lax.axis_size(axis)
    return x + lax.ppermute(x, axis, [(i, i ^ bit) for i in range(count)])


def chol_inv_kernel(g_ref, x_ref, a_ref):
    n = g_ref.shape[0]
    a_ref[...] = g_ref[...]
    rows = lax.broadcasted_iota(jnp.int32, (n, n), 0)
    cols = lax.broadcasted_iota(jnp.int32, (n, n), 1)
    x_ref[...] = jnp.where(rows == cols, 1.0, 0.0).astype(jnp.float32)
    lane = lax.broadcasted_iota(jnp.int32, (1, n), 1)
    phase = 16 if n % 16 == 0 else n

    for lo in range(0, n, phase):
        cols_lo = lax.broadcasted_iota(jnp.int32, (n - lo, n), 1)
        sub = lo + lax.broadcasted_iota(jnp.int32, (n - lo, 1), 0)

        def step(k, carry):
            a = a_ref[lo:, :]
            row = a_ref[pl.ds(k, 1), :]
            pivot = jnp.sum(jnp.where(lane == k, row, 0.0), axis=1, keepdims=True)
            scale = 1.0 / jnp.sqrt(pivot)
            col = jnp.sum(jnp.where(cols_lo == k, a, 0.0), axis=1, keepdims=True)
            below = jnp.where(sub > k, col * scale, 0.0)
            right = jnp.where(lane > k, row * scale, 0.0)
            a_ref[lo:, :] = a - below * right
            xrow = x_ref[pl.ds(k, 1), :] * scale
            x_ref[pl.ds(k, 1), :] = xrow
            x_ref[lo:, :] = x_ref[lo:, :] - below * xrow
            return carry

        lax.fori_loop(lo, min(lo + phase, n), step, 0)


def lower_inverse(gram):
    n = gram.shape[0]
    return pl.pallas_call(
        chol_inv_kernel,
        out_shape=jax.ShapeDtypeStruct((n, n), jnp.float32),
        scratch_shapes=[pltpu.VMEM((n, n), jnp.float32)],
    )(gram)


def invert_beside(gram, extra, bits):
    solved = lower_inverse(gram)
    if bits:
        extra = exchange(extra, *bits.pop(0))
    solved, extra = lax.optimization_barrier((solved, extra))
    inverse = jnp.dot(solved.T, solved, precision=lax.Precision.HIGHEST)
    return inverse, extra


def body(perturbations, trajectory):
    width = 2 * STEPS
    rows = perturbations.shape[2]
    assert width <= rows
    coeffs = halo(trajectory, width, 3).astype(jnp.float32)
    v = lax.all_to_all(perturbations, "mem", 1, 0, tiled=True)
    members = v.shape[0]
    ncells_all = (
        perturbations.shape[1]
        * perturbations.shape[2]
        * perturbations.shape[3]
        * lax.axis_size("dom")
    )
    hi = lax.Precision.HIGHEST
    flat_v = v.reshape(members, -1)
    gram = jnp.dot(flat_v, flat_v.T, precision=hi)
    pending = butterfly_bits()
    done = []

    def tick(acc, field):
        if pending:
            bit = pending.pop(0)
            acc = exchange(acc, *bit)
            done.append(bit)
        return lax.optimization_barrier((acc, field))

    field = halo(v, width, 2)
    for step in range(STEPS):
        gram, field = tick(gram, forward_step(field, coeffs[step]))
    flat_z = field[:, :, width : width + rows, :].reshape(members, -1)
    cross = jnp.dot(flat_z, flat_z.T, precision=hi)
    both = jnp.stack([gram, cross])
    cross_bits = list(done)
    for step in reversed(range(STEPS)):
        both, field = tick(both, adjoint_step(field, coeffs[step]))
    while pending:
        both = exchange(both, *pending.pop(0))
    gram, cross = both[0], both[1]
    field = field[:, :, width : width + rows, :]
    flat_w = field.reshape(members, -1)
    inverse, cross = invert_beside(gram / ncells_all, cross, cross_bits)
    ritz = jnp.dot(inverse, flat_w, precision=hi)
    for axis, bit in cross_bits:
        cross = exchange(cross, axis, bit)
    projected = cross / ncells_all
    ritz = lax.all_to_all(ritz.reshape(v.shape), "mem", 0, 1, tiled=True)
    return (ritz, projected)


def solution(mesh):
    return jax.shard_map(
        body,
        mesh=mesh,
        in_specs=(P("mem", None, "dom", None), P(None, None, "mem", "dom", None)),
        out_specs=(P("mem", None, "dom", None), P()),
        check_vma=False,
    )
```

```python
import jax
import jax.numpy as jnp
from jax import lax
from jax.experimental import pallas as pl
from jax.experimental.pallas import tpu as pltpu
from jax.sharding import PartitionSpec as P

STEPS = 2


def halo(block, width, dim):
    count = lax.axis_size("dom")
    forward = [(i, i + 1) for i in range(count - 1)]
    backward = [(i + 1, i) for i in range(count - 1)]
    size = block.shape[dim]
    low = lax.ppermute(lax.slice_in_dim(block, size - width, size, axis=dim), "dom", forward)
    high = lax.ppermute(lax.slice_in_dim(block, 0, width, axis=dim), "dom", backward)
    return jnp.concatenate([low, block, high], axis=dim)


def shifted(x, offset, dim):
    pad = [(0, 0)] * x.ndim
    size = x.shape[dim]
    if offset > 0:
        pad[dim] = (0, offset)
        return lax.slice_in_dim(jnp.pad(x, pad), offset, offset + size, axis=dim)
    pad[dim] = (-offset, 0)
    return lax.slice_in_dim(jnp.pad(x, pad), 0, size, axis=dim)


def forward_step(field, coef):
    result = coef[0] * field + coef[1] * shifted(field, -1, 2) + coef[2] * shifted(field, 1, 2)
    return result + coef[3] * shifted(field, -1, 3) + coef[4] * shifted(field, 1, 3)


def adjoint_step(field, coef):
    result = coef[0] * field + shifted(coef[1] * field, 1, 2) + shifted(coef[2] * field, -1, 2)
    return result + shifted(coef[3] * field, 1, 3) + shifted(coef[4] * field, -1, 3)


def butterfly_bits():
    rings = {"mem": (2,), "dom": (4,)}
    bits = []
    for axis in ("mem", "dom"):
        bit = 1
        while bit < lax.axis_size(axis):
            mask = bit | (bit // 2) if bit in rings[axis] else bit
            bits.append((axis, mask))
            bit *= 2
    return bits


def exchange(x, axis, bit):
    count = lax.axis_size(axis)
    return x + lax.ppermute(x, axis, [(i, i ^ bit) for i in range(count)])


def chol_inv_kernel(g_ref, x_ref, a_ref):
    n = g_ref.shape[0]
    a_ref[...] = g_ref[...]
    rows = lax.broadcasted_iota(jnp.int32, (n, n), 0)
    cols = lax.broadcasted_iota(jnp.int32, (n, n), 1)
    x_ref[...] = jnp.where(rows == cols, 1.0, 0.0).astype(jnp.float32)
    lane = lax.broadcasted_iota(jnp.int32, (1, n), 1)
    phase = 16 if n % 16 == 0 else n

    for lo in range(0, n, phase):
        cols_lo = lax.broadcasted_iota(jnp.int32, (n - lo, n), 1)
        sub = lo + lax.broadcasted_iota(jnp.int32, (n - lo, 1), 0)

        def step(k, carry):
            a = a_ref[lo:, :]
            row = a_ref[k : k + 1, :]
            pivot = jnp.sum(jnp.where(lane == k, row, 0.0), axis=1, keepdims=True)
            scale = 1.0 / jnp.sqrt(pivot)
            col = jnp.sum(jnp.where(cols_lo == k, a, 0.0), axis=1, keepdims=True)
            below = jnp.where(sub > k, col * scale, 0.0)
            right = jnp.where(lane > k, row * scale, 0.0)
            a_ref[lo:, :] = a - below * right
            xrow = x_ref[k : k + 1, :] * scale
            x_ref[k : k + 1, :] = xrow
            x_ref[lo:, :] = x_ref[lo:, :] - below * xrow
            return carry

        for k in range(lo, min(lo + phase, n)):
            step(k, 0)


def lower_inverse(gram):
    n = gram.shape[0]
    return pl.pallas_call(
        chol_inv_kernel,
        out_shape=jax.ShapeDtypeStruct((n, n), jnp.float32),
        scratch_shapes=[pltpu.VMEM((n, n), jnp.float32)],
    )(gram)


def invert_beside(gram, extra, bits):
    solved = lower_inverse(gram)
    if bits:
        extra = exchange(extra, *bits.pop(0))
    solved, extra = lax.optimization_barrier((solved, extra))
    inverse = jnp.dot(solved.T, solved, precision=lax.Precision.HIGHEST)
    return inverse, extra


def body(perturbations, trajectory):
    width = 2 * STEPS
    rows = perturbations.shape[2]
    assert width <= rows
    coeffs = halo(trajectory, width, 3).astype(jnp.float32)
    v = lax.all_to_all(perturbations, "mem", 1, 0, tiled=True)
    members = v.shape[0]
    ncells_all = (
        perturbations.shape[1]
        * perturbations.shape[2]
        * perturbations.shape[3]
        * lax.axis_size("dom")
    )
    hi = lax.Precision.HIGHEST
    flat_v = v.reshape(members, -1)
    gram = jnp.dot(flat_v, flat_v.T, precision=hi)
    pending = butterfly_bits()
    done = []

    def tick(acc, field):
        if pending:
            bit = pending.pop(0)
            acc = exchange(acc, *bit)
            done.append(bit)
        return lax.optimization_barrier((acc, field))

    field = halo(v, width, 2)
    for step in range(STEPS):
        gram, field = tick(gram, forward_step(field, coeffs[step]))
    flat_z = field[:, :, width : width + rows, :].reshape(members, -1)
    cross = jnp.dot(flat_z, flat_z.T, precision=hi)
    both = jnp.stack([gram, cross])
    cross_bits = list(done)
    for step in reversed(range(STEPS)):
        both, field = tick(both, adjoint_step(field, coeffs[step]))
    while pending:
        both = exchange(both, *pending.pop(0))
    gram, cross = both[0], both[1]
    field = field[:, :, width : width + rows, :]
    flat_w = field.reshape(members, -1)
    inverse, cross = invert_beside(gram / ncells_all, cross, cross_bits)
    ritz = jnp.dot(inverse, flat_w, precision=hi)
    for axis, bit in cross_bits:
        cross = exchange(cross, axis, bit)
    projected = cross / ncells_all
    ritz = lax.all_to_all(ritz.reshape(v.shape), "mem", 0, 1, tiled=True)
    return (ritz, projected)


def solution(mesh):
    return jax.shard_map(
        body,
        mesh=mesh,
        in_specs=(P("mem", None, "dom", None), P(None, None, "mem", "dom", None)),
        out_specs=(P("mem", None, "dom", None), P()),
        check_vma=False,
    )
```

```python
import jax
import jax.numpy as jnp
from jax import lax
from jax.experimental import pallas as pl
from jax.experimental.pallas import tpu as pltpu
from jax.sharding import PartitionSpec as P

STEPS = 2


def halo(block, width, dim):
    count = lax.axis_size("dom")
    forward = [(i, i + 1) for i in range(count - 1)]
    backward = [(i + 1, i) for i in range(count - 1)]
    size = block.shape[dim]
    low = lax.ppermute(lax.slice_in_dim(block, size - width, size, axis=dim), "dom", forward)
    high = lax.ppermute(lax.slice_in_dim(block, 0, width, axis=dim), "dom", backward)
    return jnp.concatenate([low, block, high], axis=dim)


def shifted(x, offset, dim):
    pad = [(0, 0)] * x.ndim
    size = x.shape[dim]
    if offset > 0:
        pad[dim] = (0, offset)
        return lax.slice_in_dim(jnp.pad(x, pad), offset, offset + size, axis=dim)
    pad[dim] = (-offset, 0)
    return lax.slice_in_dim(jnp.pad(x, pad), 0, size, axis=dim)


def forward_step(field, coef):
    result = coef[0] * field + coef[1] * shifted(field, -1, 2) + coef[2] * shifted(field, 1, 2)
    return result + coef[3] * shifted(field, -1, 3) + coef[4] * shifted(field, 1, 3)


def adjoint_step(field, coef):
    result = coef[0] * field + shifted(coef[1] * field, 1, 2) + shifted(coef[2] * field, -1, 2)
    return result + shifted(coef[3] * field, 1, 3) + shifted(coef[4] * field, -1, 3)


def butterfly_bits():
    rings = {"mem": (2,), "dom": (4,)}
    bits = []
    for axis in ("mem", "dom"):
        bit = 1
        while bit < lax.axis_size(axis):
            mask = bit | (bit // 2) if bit in rings[axis] else bit
            bits.append((axis, mask))
            bit *= 2
    return bits


def exchange(x, axis, bit):
    count = lax.axis_size(axis)
    return x + lax.ppermute(x, axis, [(i, i ^ bit) for i in range(count)])


def chol_inv_kernel(g_ref, x_ref, a_ref):
    n = g_ref.shape[0]
    a_ref[...] = g_ref[...]
    rows = lax.broadcasted_iota(jnp.int32, (n, n), 0)
    cols = lax.broadcasted_iota(jnp.int32, (n, n), 1)
    x_ref[...] = jnp.where(rows == cols, 1.0, 0.0).astype(jnp.float32)
    lane = lax.broadcasted_iota(jnp.int32, (1, n), 1)
    phase = 16 if n % 16 == 0 else n

    for lo in range(0, n, phase):
        cols_lo = lax.broadcasted_iota(jnp.int32, (n - lo, n), 1)
        sub = lo + lax.broadcasted_iota(jnp.int32, (n - lo, 1), 0)

        def step(k, carry):
            a = a_ref[lo:, :]
            row = a_ref[k : k + 1, :]
            pivot = jnp.sum(jnp.where(lane == k, row, 0.0), axis=1, keepdims=True)
            scale = lax.rsqrt(pivot)
            col = jnp.sum(jnp.where(cols_lo == k, a, 0.0), axis=1, keepdims=True)
            below = jnp.where(sub > k, col * scale, 0.0)
            right = jnp.where(lane > k, row * scale, 0.0)
            a_ref[lo:, :] = a - below * right
            xrow = x_ref[k : k + 1, :] * scale
            x_ref[k : k + 1, :] = xrow
            x_ref[lo:, :] = x_ref[lo:, :] - below * xrow
            return carry

        for k in range(lo, min(lo + phase, n)):
            step(k, 0)


def lower_inverse(gram):
    n = gram.shape[0]
    return pl.pallas_call(
        chol_inv_kernel,
        out_shape=jax.ShapeDtypeStruct((n, n), jnp.float32),
        scratch_shapes=[pltpu.VMEM((n, n), jnp.float32)],
    )(gram)


def invert_beside(gram, extra, bits):
    solved = lower_inverse(gram)
    if bits:
        extra = exchange(extra, *bits.pop(0))
    solved, extra = lax.optimization_barrier((solved, extra))
    inverse = jnp.dot(solved.T, solved, precision=lax.Precision.HIGHEST)
    return inverse, extra


def body(perturbations, trajectory):
    width = 2 * STEPS
    rows = perturbations.shape[2]
    assert width <= rows
    coeffs = halo(trajectory, width, 3).astype(jnp.float32)
    v = lax.all_to_all(perturbations, "mem", 1, 0, tiled=True)
    members = v.shape[0]
    ncells_all = (
        perturbations.shape[1]
        * perturbations.shape[2]
        * perturbations.shape[3]
        * lax.axis_size("dom")
    )
    hi = lax.Precision.HIGHEST
    flat_v = v.reshape(members, -1)
    gram = jnp.dot(flat_v, flat_v.T, precision=hi)
    pending = butterfly_bits()
    done = []

    def tick(acc, field):
        if pending:
            bit = pending.pop(0)
            acc = exchange(acc, *bit)
            done.append(bit)
        return lax.optimization_barrier((acc, field))

    field = halo(v, width, 2)
    for step in range(STEPS):
        gram, field = tick(gram, forward_step(field, coeffs[step]))
    flat_z = field[:, :, width : width + rows, :].reshape(members, -1)
    cross = jnp.dot(flat_z, flat_z.T, precision=hi)
    both = jnp.stack([gram, cross])
    cross_bits = list(done)
    for step in reversed(range(STEPS)):
        both, field = tick(both, adjoint_step(field, coeffs[step]))
    while pending:
        both = exchange(both, *pending.pop(0))
    gram, cross = both[0], both[1]
    field = field[:, :, width : width + rows, :]
    flat_w = field.reshape(members, -1)
    inverse, cross = invert_beside(gram / ncells_all, cross, cross_bits)
    ritz = jnp.dot(inverse, flat_w, precision=hi)
    for axis, bit in cross_bits:
        cross = exchange(cross, axis, bit)
    projected = cross / ncells_all
    ritz = lax.all_to_all(ritz.reshape(v.shape), "mem", 0, 1, tiled=True)
    return (ritz, projected)


def solution(mesh):
    return jax.shard_map(
        body,
        mesh=mesh,
        in_specs=(P("mem", None, "dom", None), P(None, None, "mem", "dom", None)),
        out_specs=(P("mem", None, "dom", None), P()),
        check_vma=False,
    )
```

```python
import jax
import jax.numpy as jnp
from jax import lax
from jax.experimental import pallas as pl
from jax.experimental.pallas import tpu as pltpu
from jax.sharding import PartitionSpec as P

STEPS = 2


def halo(block, width, dim):
    count = lax.axis_size("dom")
    forward = [(i, i + 1) for i in range(count - 1)]
    backward = [(i + 1, i) for i in range(count - 1)]
    size = block.shape[dim]
    low = lax.ppermute(lax.slice_in_dim(block, size - width, size, axis=dim), "dom", forward)
    high = lax.ppermute(lax.slice_in_dim(block, 0, width, axis=dim), "dom", backward)
    return jnp.concatenate([low, block, high], axis=dim)


def shifted(x, offset, dim):
    pad = [(0, 0)] * x.ndim
    size = x.shape[dim]
    if offset > 0:
        pad[dim] = (0, offset)
        return lax.slice_in_dim(jnp.pad(x, pad), offset, offset + size, axis=dim)
    pad[dim] = (-offset, 0)
    return lax.slice_in_dim(jnp.pad(x, pad), 0, size, axis=dim)


def forward_step(field, coef):
    result = coef[0] * field + coef[1] * shifted(field, -1, 2) + coef[2] * shifted(field, 1, 2)
    return result + coef[3] * shifted(field, -1, 3) + coef[4] * shifted(field, 1, 3)


def adjoint_step(field, coef):
    result = coef[0] * field + shifted(coef[1] * field, 1, 2) + shifted(coef[2] * field, -1, 2)
    return result + shifted(coef[3] * field, 1, 3) + shifted(coef[4] * field, -1, 3)


def butterfly_bits():
    rings = {"mem": (2,), "dom": (4,)}
    bits = []
    for axis in ("mem", "dom"):
        bit = 1
        while bit < lax.axis_size(axis):
            mask = bit | (bit // 2) if bit in rings[axis] else bit
            bits.append((axis, mask))
            bit *= 2
    return bits


def exchange(x, axis, bit):
    count = lax.axis_size(axis)
    return x + lax.ppermute(x, axis, [(i, i ^ bit) for i in range(count)])


def chol_inv_kernel(g_ref, x_ref, a_ref):
    n = g_ref.shape[0]
    a_ref[...] = g_ref[...]
    rows = lax.broadcasted_iota(jnp.int32, (n, n), 0)
    cols = lax.broadcasted_iota(jnp.int32, (n, n), 1)
    x_ref[...] = jnp.where(rows == cols, 1.0, 0.0).astype(jnp.float32)
    lane = lax.broadcasted_iota(jnp.int32, (1, n), 1)
    phase = 16 if n % 16 == 0 else n

    for lo in range(0, n, phase):
        cols_lo = lax.broadcasted_iota(jnp.int32, (n - lo, n), 1)
        sub = lo + lax.broadcasted_iota(jnp.int32, (n - lo, 1), 0)

        def step(k, carry):
            a = a_ref[lo:, :]
            row = a_ref[k : k + 1, :]
            pivot = jnp.sum(jnp.where(lane == k, row, 0.0), axis=1, keepdims=True)
            scale = lax.rsqrt(pivot)
            inv_pivot = scale * scale
            col = jnp.sum(jnp.where(cols_lo == k, a, 0.0), axis=1, keepdims=True)
            below = jnp.where(sub > k, col, 0.0)
            a_ref[lo:, :] = a - (col * row) * inv_pivot
            xrow = x_ref[k : k + 1, :]
            x_ref[lo:, :] = x_ref[lo:, :] - (below * xrow) * inv_pivot
            x_ref[k : k + 1, :] = xrow * scale
            return carry

        for k in range(lo, min(lo + phase, n)):
            step(k, 0)


def lower_inverse(gram):
    n = gram.shape[0]
    return pl.pallas_call(
        chol_inv_kernel,
        out_shape=jax.ShapeDtypeStruct((n, n), jnp.float32),
        scratch_shapes=[pltpu.VMEM((n, n), jnp.float32)],
    )(gram)


def invert_beside(gram, extra, bits):
    solved = lower_inverse(gram)
    if bits:
        extra = exchange(extra, *bits.pop(0))
    solved, extra = lax.optimization_barrier((solved, extra))
    inverse = jnp.dot(solved.T, solved, precision=lax.Precision.HIGHEST)
    return inverse, extra


def body(perturbations, trajectory):
    width = 2 * STEPS
    rows = perturbations.shape[2]
    assert width <= rows
    coeffs = halo(trajectory, width, 3).astype(jnp.float32)
    v = lax.all_to_all(perturbations, "mem", 1, 0, tiled=True)
    members = v.shape[0]
    ncells_all = (
        perturbations.shape[1]
        * perturbations.shape[2]
        * perturbations.shape[3]
        * lax.axis_size("dom")
    )
    hi = lax.Precision.HIGHEST
    flat_v = v.reshape(members, -1)
    gram = jnp.dot(flat_v, flat_v.T, precision=hi)
    pending = butterfly_bits()
    done = []

    def tick(acc, field):
        if pending:
            bit = pending.pop(0)
            acc = exchange(acc, *bit)
            done.append(bit)
        return lax.optimization_barrier((acc, field))

    field = halo(v, width, 2)
    for step in range(STEPS):
        gram, field = tick(gram, forward_step(field, coeffs[step]))
    flat_z = field[:, :, width : width + rows, :].reshape(members, -1)
    cross = jnp.dot(flat_z, flat_z.T, precision=hi)
    both = jnp.stack([gram, cross])
    cross_bits = list(done)
    for step in reversed(range(STEPS)):
        both, field = tick(both, adjoint_step(field, coeffs[step]))
    while pending:
        both = exchange(both, *pending.pop(0))
    gram, cross = both[0], both[1]
    field = field[:, :, width : width + rows, :]
    flat_w = field.reshape(members, -1)
    inverse, cross = invert_beside(gram / ncells_all, cross, cross_bits)
    ritz = jnp.dot(inverse, flat_w, precision=hi)
    for axis, bit in cross_bits:
        cross = exchange(cross, axis, bit)
    projected = cross / ncells_all
    ritz = lax.all_to_all(ritz.reshape(v.shape), "mem", 0, 1, tiled=True)
    return (ritz, projected)


def solution(mesh):
    return jax.shard_map(
        body,
        mesh=mesh,
        in_specs=(P("mem", None, "dom", None), P(None, None, "mem", "dom", None)),
        out_specs=(P("mem", None, "dom", None), P()),
        check_vma=False,
    )
```

```python
import jax
import jax.numpy as jnp
from jax import lax
from jax.experimental import pallas as pl
from jax.experimental.pallas import tpu as pltpu
from jax.sharding import PartitionSpec as P

STEPS = 2


def halo(block, width, dim):
    count = lax.axis_size("dom")
    forward = [(i, i + 1) for i in range(count - 1)]
    backward = [(i + 1, i) for i in range(count - 1)]
    size = block.shape[dim]
    low = lax.ppermute(lax.slice_in_dim(block, size - width, size, axis=dim), "dom", forward)
    high = lax.ppermute(lax.slice_in_dim(block, 0, width, axis=dim), "dom", backward)
    return jnp.concatenate([low, block, high], axis=dim)


def shifted(x, offset, dim):
    pad = [(0, 0)] * x.ndim
    size = x.shape[dim]
    if offset > 0:
        pad[dim] = (0, offset)
        return lax.slice_in_dim(jnp.pad(x, pad), offset, offset + size, axis=dim)
    pad[dim] = (-offset, 0)
    return lax.slice_in_dim(jnp.pad(x, pad), 0, size, axis=dim)


def forward_step(field, coef):
    result = coef[0] * field + coef[1] * shifted(field, -1, 2) + coef[2] * shifted(field, 1, 2)
    return result + coef[3] * shifted(field, -1, 3) + coef[4] * shifted(field, 1, 3)


def adjoint_step(field, coef):
    result = coef[0] * field + shifted(coef[1] * field, 1, 2) + shifted(coef[2] * field, -1, 2)
    return result + shifted(coef[3] * field, 1, 3) + shifted(coef[4] * field, -1, 3)


def butterfly_bits():
    rings = {"mem": (2,), "dom": (4,)}
    bits = []
    for axis in ("mem", "dom"):
        bit = 1
        while bit < lax.axis_size(axis):
            mask = bit | (bit // 2) if bit in rings[axis] else bit
            bits.append((axis, mask))
            bit *= 2
    return bits


def exchange(x, axis, bit):
    count = lax.axis_size(axis)
    return x + lax.ppermute(x, axis, [(i, i ^ bit) for i in range(count)])


def chol_inv_kernel(g_ref, x_ref, a_ref):
    n = g_ref.shape[0]
    a_ref[...] = g_ref[...]
    rows = lax.broadcasted_iota(jnp.int32, (n, n), 0)
    cols = lax.broadcasted_iota(jnp.int32, (n, n), 1)
    x_ref[...] = jnp.where(rows == cols, 1.0, 0.0).astype(jnp.float32)
    lane = lax.broadcasted_iota(jnp.int32, (1, n), 1)
    phase = 16 if n % 16 == 0 else n

    for lo in range(0, n, phase):
        cols_lo = lax.broadcasted_iota(jnp.int32, (n - lo, n), 1)
        sub = lo + lax.broadcasted_iota(jnp.int32, (n - lo, 1), 0)

        def step(k, carry):
            a = a_ref[lo:, :]
            row = a_ref[k : k + 1, :]
            pivot = jnp.sum(jnp.where(lane == k, row, 0.0), axis=1, keepdims=True)
            scale = lax.rsqrt(pivot)
            col = jnp.sum(jnp.where(cols_lo == k, a, 0.0), axis=1, keepdims=True)
            below = jnp.where(sub > k, col * scale, 0.0)
            right = jnp.where(lane > k, row * scale, 0.0)
            a_ref[lo:, :] = a - below * right
            xrow = x_ref[k : k + 1, :] * scale
            x_ref[k : k + 1, :] = xrow
            x_ref[lo:, :] = x_ref[lo:, :] - below * xrow
            return carry

        for k in range(lo, min(lo + phase, n)):
            step(k, 0)


def inverse_kernel(g_ref, o_ref, x_ref, a_ref):
    chol_inv_kernel(g_ref, x_ref, a_ref)
    x = x_ref[...]
    o_ref[...] = lax.dot_general(
        x, x, (((0,), (0,)), ((), ())), precision=lax.Precision.HIGHEST,
        preferred_element_type=jnp.float32,
    )


def invert_beside(gram, extra, bits):
    n = gram.shape[0]
    inverse = pl.pallas_call(
        inverse_kernel,
        out_shape=jax.ShapeDtypeStruct((n, n), jnp.float32),
        scratch_shapes=[pltpu.VMEM((n, n), jnp.float32), pltpu.VMEM((n, n), jnp.float32)],
    )(gram)
    if bits:
        extra = exchange(extra, *bits.pop(0))
    inverse, extra = lax.optimization_barrier((inverse, extra))
    return inverse, extra


def body(perturbations, trajectory):
    width = 2 * STEPS
    rows = perturbations.shape[2]
    assert width <= rows
    coeffs = halo(trajectory, width, 3).astype(jnp.float32)
    v = lax.all_to_all(perturbations, "mem", 1, 0, tiled=True)
    members = v.shape[0]
    ncells_all = (
        perturbations.shape[1]
        * perturbations.shape[2]
        * perturbations.shape[3]
        * lax.axis_size("dom")
    )
    hi = lax.Precision.HIGHEST
    flat_v = v.reshape(members, -1)
    gram = jnp.dot(flat_v, flat_v.T, precision=hi)
    pending = butterfly_bits()
    done = []

    def tick(acc, field):
        if pending:
            bit = pending.pop(0)
            acc = exchange(acc, *bit)
            done.append(bit)
        return lax.optimization_barrier((acc, field))

    field = halo(v, width, 2)
    for step in range(STEPS):
        gram, field = tick(gram, forward_step(field, coeffs[step]))
    flat_z = field[:, :, width : width + rows, :].reshape(members, -1)
    cross = jnp.dot(flat_z, flat_z.T, precision=hi)
    both = jnp.stack([gram, cross])
    cross_bits = list(done)
    for step in reversed(range(STEPS)):
        both, field = tick(both, adjoint_step(field, coeffs[step]))
    while pending:
        both = exchange(both, *pending.pop(0))
    gram, cross = both[0], both[1]
    field = field[:, :, width : width + rows, :]
    flat_w = field.reshape(members, -1)
    inverse, cross = invert_beside(gram / ncells_all, cross, cross_bits)
    ritz = jnp.dot(inverse, flat_w, precision=hi)
    for axis, bit in cross_bits:
        cross = exchange(cross, axis, bit)
    projected = cross / ncells_all
    ritz = lax.all_to_all(ritz.reshape(v.shape), "mem", 0, 1, tiled=True)
    return (ritz, projected)


def solution(mesh):
    return jax.shard_map(
        body,
        mesh=mesh,
        in_specs=(P("mem", None, "dom", None), P(None, None, "mem", "dom", None)),
        out_specs=(P("mem", None, "dom", None), P()),
        check_vma=False,
    )
```

```python
import jax
import jax.numpy as jnp
from jax import lax
from jax.experimental import pallas as pl
from jax.experimental.pallas import tpu as pltpu
from jax.sharding import PartitionSpec as P

STEPS = 2


def halo(block, width, dim):
    count = lax.axis_size("dom")
    forward = [(i, i + 1) for i in range(count - 1)]
    backward = [(i + 1, i) for i in range(count - 1)]
    size = block.shape[dim]
    low = lax.ppermute(lax.slice_in_dim(block, size - width, size, axis=dim), "dom", forward)
    high = lax.ppermute(lax.slice_in_dim(block, 0, width, axis=dim), "dom", backward)
    return jnp.concatenate([low, block, high], axis=dim)


def shifted(x, offset, dim):
    pad = [(0, 0)] * x.ndim
    size = x.shape[dim]
    if offset > 0:
        pad[dim] = (0, offset)
        return lax.slice_in_dim(jnp.pad(x, pad), offset, offset + size, axis=dim)
    pad[dim] = (-offset, 0)
    return lax.slice_in_dim(jnp.pad(x, pad), 0, size, axis=dim)


def forward_step(field, coef):
    result = coef[0] * field + coef[1] * shifted(field, -1, 2) + coef[2] * shifted(field, 1, 2)
    return result + coef[3] * shifted(field, -1, 3) + coef[4] * shifted(field, 1, 3)


def adjoint_step(field, coef):
    result = coef[0] * field + shifted(coef[1] * field, 1, 2) + shifted(coef[2] * field, -1, 2)
    return result + shifted(coef[3] * field, 1, 3) + shifted(coef[4] * field, -1, 3)


def butterfly_bits():
    rings = {"mem": (2,), "dom": (4,)}
    bits = []
    for axis in ("mem", "dom"):
        bit = 1
        while bit < lax.axis_size(axis):
            mask = bit | (bit // 2) if bit in rings[axis] else bit
            bits.append((axis, mask))
            bit *= 2
    return bits


def exchange(x, axis, bit):
    count = lax.axis_size(axis)
    return x + lax.ppermute(x, axis, [(i, i ^ bit) for i in range(count)])


def chol_inv_kernel(g_ref, x_ref, a_ref):
    n = g_ref.shape[0]
    a_ref[...] = g_ref[...]
    rows = lax.broadcasted_iota(jnp.int32, (n, n), 0)
    cols = lax.broadcasted_iota(jnp.int32, (n, n), 1)
    x_ref[...] = jnp.where(rows == cols, 1.0, 0.0).astype(jnp.float32)
    lane = lax.broadcasted_iota(jnp.int32, (1, n), 1)
    phase = 16 if n % 16 == 0 else n

    for lo in range(0, n, phase):
        cols_lo = lax.broadcasted_iota(jnp.int32, (n - lo, n), 1)
        sub = lo + lax.broadcasted_iota(jnp.int32, (n - lo, 1), 0)

        def step(k, carry):
            a = a_ref[lo:, :]
            row = a_ref[k : k + 1, :]
            pivot = jnp.sum(jnp.where(lane == k, row, 0.0), axis=1, keepdims=True)
            scale = lax.rsqrt(pivot)
            col = jnp.sum(jnp.where(cols_lo == k, a, 0.0), axis=1, keepdims=True)
            below = jnp.where(sub > k, col * scale, 0.0)
            right = jnp.where(lane > k, row * scale, 0.0)
            a_ref[lo:, :] = a - below * right
            xrow = x_ref[k : k + 1, :] * scale
            x_ref[k : k + 1, :] = xrow
            x_ref[lo:, :] = x_ref[lo:, :] - below * xrow
            return carry

        for k in range(lo, min(lo + phase, n)):
            step(k, 0)


def inverse_kernel(g_ref, o_ref, x_ref, a_ref):
    chol_inv_kernel(g_ref, x_ref, a_ref)
    x = x_ref[...]
    o_ref[...] = lax.dot_general(
        x, x, (((0,), (0,)), ((), ())), precision=lax.Precision.HIGHEST,
        preferred_element_type=jnp.float32,
    )


def invert_beside(gram, extra, bits):
    n = gram.shape[0]
    inverse = pl.pallas_call(
        inverse_kernel,
        out_shape=jax.ShapeDtypeStruct((n, n), jnp.float32),
        scratch_shapes=[pltpu.VMEM((n, n), jnp.float32), pltpu.VMEM((n, n), jnp.float32)],
    )(gram)
    if bits:
        extra = exchange(extra, *bits.pop(0))
    inverse, extra = lax.optimization_barrier((inverse, extra))
    return inverse, extra


def body(perturbations, trajectory):
    width = 2 * STEPS
    rows = perturbations.shape[2]
    assert width <= rows
    coeffs = halo(trajectory, width, 3).astype(jnp.float32)
    v = lax.all_to_all(perturbations, "mem", 1, 0, tiled=True)
    members = v.shape[0]
    ncells_all = (
        perturbations.shape[1]
        * perturbations.shape[2]
        * perturbations.shape[3]
        * lax.axis_size("dom")
    )
    hi = lax.Precision.HIGHEST
    gram = jnp.einsum("alij,blij->ab", v, v, precision=hi)
    pending = butterfly_bits()
    done = []

    def tick(acc, field):
        if pending:
            bit = pending.pop(0)
            acc = exchange(acc, *bit)
            done.append(bit)
        return lax.optimization_barrier((acc, field))

    field = halo(v, width, 2)
    for step in range(STEPS):
        gram, field = tick(gram, forward_step(field, coeffs[step]))
    own = field[:, :, width : width + rows, :]
    cross = jnp.einsum("alij,blij->ab", own, own, precision=hi)
    both = jnp.stack([gram, cross])
    cross_bits = list(done)
    for step in reversed(range(STEPS)):
        both, field = tick(both, adjoint_step(field, coeffs[step]))
    while pending:
        both = exchange(both, *pending.pop(0))
    gram, cross = both[0], both[1]
    field = field[:, :, width : width + rows, :]
    inverse, cross = invert_beside(gram / ncells_all, cross, cross_bits)
    ritz = jnp.einsum("ab,blij->alij", inverse, field, precision=hi)
    for axis, bit in cross_bits:
        cross = exchange(cross, axis, bit)
    projected = cross / ncells_all
    ritz = lax.all_to_all(ritz, "mem", 0, 1, tiled=True)
    return (ritz, projected)


def solution(mesh):
    return jax.shard_map(
        body,
        mesh=mesh,
        in_specs=(P("mem", None, "dom", None), P(None, None, "mem", "dom", None)),
        out_specs=(P("mem", None, "dom", None), P()),
        check_vma=False,
    )
```
